32 devices in a mesh: groups: 2 (over x), row: 8 (over z, y), col: 2 (over core).
Axes of the slice: x: 2, y: 2, z: 4, core: 2. Of those that a mesh axis runs over, the one named last changes fastest.
Arguments:
- sky_map: bfloat16 [512, 1024, 128], P(('groups', 'row'), 'col'), parts along dimension 0, may hold values from -6 to 6
- expand_weight: bfloat16 [128, 256], replicated, may hold values from -0.5 to 0.5
- expand_bias: float32 [256], replicated, may hold values from -3 to 3
- depth_weight: float32 [3, 3, 256], replicated, may hold values from -2 to 2
- depth_bias: float32 [256], replicated, may hold values from -3 to 3
- project_weight: bfloat16 [256, 128], replicated, may hold values from -0.375 to 0.375
- project_bias: float32 [128], replicated, may hold values from -3 to 3
- norm_gain: float32 [128], replicated, may hold values from 0.1 to 1.9
- norm_bias: float32 [128], replicated, may hold values from -3 to 3
- mixing_weight: bfloat16 [128, 384], replicated
- position_bias: float32 [4, 225], replicated, may hold values from -4 to 4
- output_weight: bfloat16 [128, 128], replicated, may hold values from -0.5 to 0.5
Outputs:
- block_out: bfloat16 [512, 1024, 128], P(('groups', 'row'), 'col'), parts along dimension 0
The draws below stay inside these ranges and needn't reach their ends.
There are 2 independent parts, one for each index of `groups`. The reference program is written for one: setup_inputs(seed, part) draws one part's arguments, and reference() takes and returns one part's arrays. A program takes and returns all parts, laid end to end along the dimension named above; an argument that names none is the same for every part. Nothing has to cross between parts.
All inputs are finite; a program needn't handle non-finite values.
Results may differ from the reference program's by a relative error of at most 0.023.
Values may be sent and summed in bfloat16 or wider, within the bound.
No kernel may reach another device: no remote copies, remote signals or barrier semaphores. Data moves between devices by JAX's collectives and lax.ppermute only.
A program may use at most 128 MiB of HBM per device.

```python
import jax
import jax.numpy as jnp
from jax import lax

CH = 128
EXP_CH = 256
HEADS = 4
G = 8
MAP_ROWS = 256
MAP_COLS = 1024


def draw_mixing_weight(key, part):
    first_key = jax.random.fold_in(jax.random.fold_in(key, 7), 0)
    base = jax.random.normal(first_key, (CH, 3 * CH), jnp.float32) * CH ** (-0.5)
    return base.astype(jnp.bfloat16)


def levels(key, dims, cuts, smallest, top_value):
    loudness, own = 1.0, jax.random.fold_in(key, 6)
    for dim, blocks in cuts:
        heights = jnp.exp(jax.random.uniform(jax.random.fold_in(own, dim), (blocks,), jnp.float32, smallest / len(cuts), top_value / len(cuts)))
        loudness = loudness * jnp.repeat(heights, dims[dim] // blocks).reshape([-1 if axis == dim else 1 for axis in range(len(dims))])
    return loudness


def noise(stream_key, extent, width, most, shards=(), kind=jnp.bfloat16):
    values = jax.random.normal(stream_key, extent, jnp.float32) * width
    if len(shards) > 0:
        values = levels(stream_key, extent, shards, -0.22, 0.18) * values
    return jnp.clip(values, min=-most, max=most).astype(kind)


def setup_inputs(seed: int = 0, part: int = 0) -> dict:
    key_list = jax.random.split(jax.random.key(seed), 13)
    part_splits = jax.random.split(jax.random.fold_in(key_list[12], part), 13)
    return {
        "sky_map": noise(part_splits[0], (MAP_ROWS, MAP_COLS, CH), 1.0, 6.0, ((0, 8), (1, 2))),
        "expand_weight": noise(key_list[1], (CH, EXP_CH), CH ** -0.5, 0.5),
        "expand_bias": noise(key_list[2], (EXP_CH,), 0.5, 3.0, (), jnp.float32),
        "depth_weight": noise(key_list[3], (3, 3, EXP_CH), 9 ** -0.5, 2.0, (), jnp.float32),
        "depth_bias": noise(key_list[4], (EXP_CH,), 0.5, 3.0, (), jnp.float32),
        "project_weight": noise(key_list[5], (EXP_CH, CH), EXP_CH ** -0.5, 0.375),
        "project_bias": noise(key_list[6], (CH,), 0.5, 3.0, (), jnp.float32),
        "norm_gain": jnp.clip(1.0 + 0.18 * jax.random.normal(key_list[7], (CH,), jnp.float32), 0.1, 1.9),
        "norm_bias": noise(key_list[8], (CH,), 0.5, 3.0, (), jnp.float32),
        "mixing_weight": draw_mixing_weight(jax.random.fold_in(key_list[12], 71), part),
        "position_bias": noise(key_list[10], (HEADS, (2 * G - 1) * (2 * G - 1)), 1.0, 4.0, (), jnp.float32),
        "output_weight": noise(key_list[11], (CH, CH), CH ** -0.5, 0.5),
    }


def gelu_tanh(values):
    return jax.nn.gelu(values, approximate=True)

def expand_layer(features, expand_weight, expand_bias):
    return gelu_tanh(jnp.dot(features, expand_weight, preferred_element_type=jnp.float32) + expand_bias).astype(jnp.bfloat16)

def depthwise(padded, depth_weight, depth_bias, row_count, col_count):
    accumulated = jnp.zeros((row_count, col_count, padded.shape[2]), jnp.float32) + depth_bias
    for row_shift in range(3):
        for col_shift in range(3):
            accumulated = accumulated + padded[row_shift:row_shift + row_count, col_shift:col_shift + col_count].astype(jnp.float32) * depth_weight[row_shift, col_shift]
    return gelu_tanh(accumulated).astype(jnp.bfloat16)

def layer_norm(features, norm_gain, norm_bias):
    values = features.astype(jnp.float32)
    mean_value = lax.optimization_barrier(jnp.mean(values, axis=-1, keepdims=True))
    variance = lax.optimization_barrier(jnp.mean((values - mean_value) ** 2, axis=-1, keepdims=True))
    return ((values - mean_value) * lax.rsqrt(variance + 1e-05) * norm_gain + norm_bias).astype(jnp.bfloat16)

def grid_bias(position_bias, grid_side):
    position = jnp.arange(grid_side * grid_side, dtype=jnp.int32)
    row_of = position // grid_side
    col_of = position % grid_side
    offset_index = (row_of[:, None] - row_of[None, :] + grid_side - 1) * (2 * grid_side - 1) + (col_of[:, None] - col_of[None, :] + grid_side - 1)
    entries = jnp.arange((2 * grid_side - 1) ** 2, dtype=jnp.int32)
    one_hot = (offset_index[:, :, None] == entries[None, None, :]).astype(jnp.float32)
    return jnp.einsum('qkt,ht->hqk', one_hot, position_bias.astype(jnp.float32), precision=lax.Precision.HIGHEST)

def attend(projected, table, head_count):
    group_count, tokens, triple = projected.shape
    channels = triple // 3
    head_size = channels // head_count
    split_parts = projected.reshape(group_count, tokens, 3, head_count, head_size).astype(jnp.float32)
    query_part = split_parts[:, :, 0]
    key_part = split_parts[:, :, 1]
    value_part = split_parts[:, :, 2]
    scores = jnp.einsum('nqhd,nkhd->nhqk', query_part, key_part) * head_size ** (-0.5) + table[None]
    probs = jax.nn.softmax(scores, axis=-1).astype(jnp.bfloat16)
    attended = jnp.einsum('nhqk,nkhd->nqhd', probs.astype(jnp.float32), value_part)
    return attended.astype(jnp.bfloat16).reshape(group_count, tokens, channels)

def reference(sky_map, expand_weight, expand_bias, depth_weight, depth_bias, project_weight, project_bias, norm_gain, norm_bias, mixing_weight, position_bias, output_weight):
    map_rows, map_cols, channels = sky_map.shape
    expanded = expand_layer(sky_map, expand_weight, expand_bias)
    padded = jnp.pad(expanded, ((1, 1), (1, 1), (0, 0)))
    hidden = depthwise(padded, depth_weight, depth_bias, map_rows, map_cols)
    after_conv = (sky_map.astype(jnp.float32) + jnp.dot(hidden, project_weight, preferred_element_type=jnp.float32) + project_bias).astype(jnp.bfloat16)
    normed = layer_norm(after_conv, norm_gain, norm_bias)
    projected = jnp.dot(normed, mixing_weight, preferred_element_type=jnp.float32).astype(jnp.bfloat16)
    stride_rows = map_rows // G
    stride_cols = map_cols // G
    grouped = projected.reshape(G, stride_rows, G, stride_cols, 3 * channels).transpose(1, 3, 0, 2, 4).reshape(stride_rows, stride_cols, G * G, 3 * channels)
    table = grid_bias(position_bias, G)

    def one_block(block):
        return attend(block, table, HEADS)
    heads_out = lax.map(one_block, grouped)
    returned = heads_out.reshape(stride_rows, stride_cols, G, G, channels).transpose(2, 0, 3, 1, 4).reshape(map_rows, map_cols, channels)
    return (after_conv.astype(jnp.float32) + jnp.dot(returned, output_weight, preferred_element_type=jnp.float32)).astype(jnp.bfloat16)
```

```python
import jax
import jax.numpy as jnp
from jax import lax
from jax.sharding import PartitionSpec as P

HEADS = 4
G = 8


def with_halo(array, sides, width):
    for axis, dim in sides:
        size, length = (lax.axis_size(axis), array.shape[dim])
        up = [(i, (i + 1) % size) for i in range(size - 1)]
        down = [(j, i) for i, j in up]
        last = lax.slice_in_dim(array, length - width, length, axis=dim)
        initial = lax.slice_in_dim(array, 0, width, axis=dim)
        before = lax.ppermute(last, axis, up)
        after = lax.ppermute(initial, axis, down)
        array = jnp.concatenate([before, array, after], axis=dim)
    return array


def gelu_tanh(values):
    return jax.nn.gelu(values, approximate=True)


def expand_layer(features, expand_weight, expand_bias):
    return gelu_tanh(
        jnp.dot(features, expand_weight, preferred_element_type=jnp.float32) + expand_bias
    ).astype(jnp.bfloat16)


def depthwise(padded, depth_weight, depth_bias, row_count, col_count):
    accumulated = jnp.zeros((row_count, col_count, padded.shape[2]), jnp.float32) + depth_bias
    for row_shift in range(3):
        for col_shift in range(3):
            accumulated = (
                accumulated
                + padded[row_shift : row_shift + row_count, col_shift : col_shift + col_count]
                * depth_weight[row_shift, col_shift]
            )
    return gelu_tanh(accumulated).astype(jnp.bfloat16)


def layer_norm(features, norm_gain, norm_bias):
    values = features.astype(jnp.float32)
    mean_value = jnp.mean(values, axis=-1, keepdims=True)
    variance = jnp.mean((values - mean_value) ** 2, axis=-1, keepdims=True)
    return ((values - mean_value) * lax.rsqrt(variance + 1e-05) * norm_gain + norm_bias).astype(
        jnp.bfloat16
    )


def grid_bias(position_bias, grid_side):
    position = jnp.arange(grid_side * grid_side, dtype=jnp.int32)
    row_of = position // grid_side
    col_of = position % grid_side
    offset_index = (row_of[:, None] - row_of[None, :] + grid_side - 1) * (2 * grid_side - 1) + (
        col_of[:, None] - col_of[None, :] + grid_side - 1
    )
    return jnp.take(position_bias, offset_index, axis=1)


def attend(projected, table, head_count):
    group_count, tokens, triple = projected.shape
    channels = triple // 3
    head_size = channels // head_count
    split_parts = projected.reshape(group_count, tokens, 3, head_count, head_size)
    query_part = split_parts[:, :, 0]
    key_part = split_parts[:, :, 1]
    value_part = split_parts[:, :, 2]
    scores = (
        jnp.einsum("nqhd,nkhd->nhqk", query_part, key_part, preferred_element_type=jnp.float32)
        * head_size ** (-0.5)
        + table[None]
    )
    probs = jax.nn.softmax(scores, axis=-1).astype(jnp.bfloat16)
    attended = jnp.einsum("nhqk,nkhd->nqhd", probs, value_part, preferred_element_type=jnp.float32)
    return attended.astype(jnp.bfloat16).reshape(group_count, tokens, channels)


def body(
    sky_map,
    expand_weight,
    expand_bias,
    depth_weight,
    depth_bias,
    project_weight,
    project_bias,
    norm_gain,
    norm_bias,
    mixing_weight,
    position_bias,
    output_weight,
):
    row_count, col_count, channels = sky_map.shape
    expanded = expand_layer(sky_map, expand_weight, expand_bias)
    padded = with_halo(expanded, (("row", 0), ("col", 1)), 1)
    hidden = depthwise(padded, depth_weight, depth_bias, row_count, col_count)
    after_conv = (
        sky_map.astype(jnp.float32)
        + jnp.dot(hidden, project_weight, preferred_element_type=jnp.float32)
        + project_bias
    ).astype(jnp.bfloat16)
    normed = layer_norm(after_conv, norm_gain, norm_bias)
    across = G // lax.axis_size("col")
    stride = col_count // across
    moved = lax.all_to_all(
        lax.all_to_all(
            normed.reshape(row_count, across, stride, channels),
            "row",
            split_axis=0,
            concat_axis=0,
            tiled=True,
        ),
        "col",
        split_axis=2,
        concat_axis=1,
        tiled=True,
    )
    projected = jnp.dot(moved, mixing_weight, preferred_element_type=jnp.float32).astype(
        jnp.bfloat16
    )
    inner_rows = row_count // G
    inner_cols = projected.shape[2]
    grouped = (
        projected.reshape(G, inner_rows, G, inner_cols, 3 * channels)
        .transpose(1, 3, 0, 2, 4)
        .reshape(inner_rows, inner_cols, G * G, 3 * channels)
    )
    table = grid_bias(position_bias, G)

    def one_block(block):
        return attend(block, table, HEADS)

    heads_out = lax.map(one_block, grouped)
    returned = (
        heads_out.reshape(inner_rows, inner_cols, G, G, channels)
        .transpose(2, 0, 3, 1, 4)
        .reshape(row_count, G, inner_cols, channels)
    )
    returned = lax.all_to_all(
        lax.all_to_all(returned, "row", split_axis=0, concat_axis=0, tiled=True),
        "col",
        split_axis=1,
        concat_axis=2,
        tiled=True,
    )
    returned = returned.reshape(row_count, col_count, channels)
    return (
        after_conv.astype(jnp.float32)
        + jnp.dot(returned, output_weight, preferred_element_type=jnp.float32)
    ).astype(jnp.bfloat16)


def solution(mesh):
    placed = (
        P(("groups", "row"), "col", None),
        P(),
        P(),
        P(),
        P(),
        P(),
        P(),
        P(),
        P(),
        P(),
        P(),
        P(),
    )
    return jax.shard_map(
        body,
        mesh=mesh,
        in_specs=placed,
        out_specs=P(("groups", "row"), "col", None),
        check_vma=False,
    )
```

```python
import jax
import jax.numpy as jnp
from jax import lax
from jax.sharding import PartitionSpec as P

HEADS = 4
G = 8


def with_halo(array, sides, width):
    for axis, dim in sides:
        size, length = (lax.axis_size(axis), array.shape[dim])
        up = [(i, (i + 1) % size) for i in range(size - 1)]
        down = [(j, i) for i, j in up]
        last = lax.slice_in_dim(array, length - width, length, axis=dim)
        initial = lax.slice_in_dim(array, 0, width, axis=dim)
        before = lax.ppermute(last, axis, up)
        after = lax.ppermute(initial, axis, down)
        array = jnp.concatenate([before, array, after], axis=dim)
    return array


def gelu_tanh(values):
    return jax.nn.gelu(values, approximate=True)


def expand_layer(features, expand_weight, expand_bias):
    return gelu_tanh(
        jnp.dot(features, expand_weight, preferred_element_type=jnp.float32) + expand_bias
    ).astype(jnp.bfloat16)


def depthwise(padded, depth_weight, depth_bias, row_count, col_count):
    accumulated = jnp.zeros((row_count, col_count, padded.shape[2]), jnp.float32) + depth_bias
    for row_shift in range(3):
        for col_shift in range(3):
            accumulated = (
                accumulated
                + padded[row_shift : row_shift + row_count, col_shift : col_shift + col_count]
                * depth_weight[row_shift, col_shift]
            )
    return gelu_tanh(accumulated).astype(jnp.bfloat16)


def layer_norm(features, norm_gain, norm_bias):
    values = features.astype(jnp.float32)
    mean_value = jnp.mean(values, axis=-1, keepdims=True)
    variance = jnp.mean((values - mean_value) ** 2, axis=-1, keepdims=True)
    return ((values - mean_value) * lax.rsqrt(variance + 1e-05) * norm_gain + norm_bias).astype(
        jnp.bfloat16
    )


def grid_bias(position_bias, grid_side):
    position = jnp.arange(grid_side * grid_side, dtype=jnp.int32)
    row_of = position // grid_side
    col_of = position % grid_side
    offset_index = (row_of[:, None] - row_of[None, :] + grid_side - 1) * (2 * grid_side - 1) + (
        col_of[:, None] - col_of[None, :] + grid_side - 1
    )
    return jnp.take(position_bias, offset_index, axis=1)


def attend(projected, table, head_count):
    group_count, tokens, triple = projected.shape
    channels = triple // 3
    head_size = channels // head_count
    split_parts = projected.reshape(group_count, tokens, 3, head_count, head_size)
    query_part = split_parts[:, :, 0]
    key_part = split_parts[:, :, 1]
    value_part = split_parts[:, :, 2]
    scores = (
        jnp.einsum("nqhd,nkhd->nhqk", query_part, key_part, preferred_element_type=jnp.float32)
        * head_size ** (-0.5)
        + table[None]
    )
    probs = jax.nn.softmax(scores, axis=-1).astype(jnp.bfloat16)
    attended = jnp.einsum("nhqk,nkhd->nqhd", probs, value_part, preferred_element_type=jnp.float32)
    return attended.astype(jnp.bfloat16).reshape(group_count, tokens, channels)


def body(
    sky_map,
    expand_weight,
    expand_bias,
    depth_weight,
    depth_bias,
    project_weight,
    project_bias,
    norm_gain,
    norm_bias,
    mixing_weight,
    position_bias,
    output_weight,
):
    row_count, col_count, channels = sky_map.shape
    row_size = lax.axis_size("row")
    expanded = expand_layer(sky_map, expand_weight, expand_bias)
    padded = with_halo(expanded, (("row", 0), ("col", 1)), 1)
    across = G // lax.axis_size("col")
    stride = col_count // across
    table = grid_bias(position_bias, G)
    pieces = 2 if row_count % (2 * row_size) == 0 and (row_count // 2) % G == 0 else 1
    span = row_count // pieces
    outs = []
    for piece in range(pieces):
        first = piece * span
        hidden = depthwise(padded[first : first + span + 2], depth_weight, depth_bias, span, col_count)
        after_conv = (
            sky_map[first : first + span].astype(jnp.float32)
            + jnp.dot(hidden, project_weight, preferred_element_type=jnp.float32)
            + project_bias
        ).astype(jnp.bfloat16)
        normed = layer_norm(after_conv, norm_gain, norm_bias)
        moved = lax.all_to_all(
            lax.all_to_all(
                normed.reshape(span, across, stride, channels),
                "row",
                split_axis=0,
                concat_axis=0,
                tiled=True,
            ),
            "col",
            split_axis=2,
            concat_axis=1,
            tiled=True,
        )
        projected = jnp.dot(moved, mixing_weight, preferred_element_type=jnp.float32).astype(
            jnp.bfloat16
        )
        inner_rows = span // G
        inner_cols = projected.shape[2]
        grouped = (
            projected.reshape(G, inner_rows, G, inner_cols, 3 * channels)
            .transpose(1, 3, 0, 2, 4)
            .reshape(inner_rows * inner_cols, G * G, 3 * channels)
        )
        heads_out = attend(grouped, table, HEADS)
        returned = (
            heads_out.reshape(inner_rows, inner_cols, G, G, channels)
            .transpose(2, 0, 3, 1, 4)
            .reshape(span, G, inner_cols, channels)
        )
        returned = lax.all_to_all(
            lax.all_to_all(returned, "row", split_axis=0, concat_axis=0, tiled=True),
            "col",
            split_axis=1,
            concat_axis=2,
            tiled=True,
        )
        returned = returned.reshape(span, col_count, channels)
        outs.append(
            (
                after_conv.astype(jnp.float32)
                + jnp.dot(returned, output_weight, preferred_element_type=jnp.float32)
            ).astype(jnp.bfloat16)
        )
    return jnp.concatenate(outs, axis=0)


def solution(mesh):
    placed = (
        P(("groups", "row"), "col", None),
        P(),
        P(),
        P(),
        P(),
        P(),
        P(),
        P(),
        P(),
        P(),
        P(),
        P(),
    )
    return jax.shard_map(
        body,
        mesh=mesh,
        in_specs=placed,
        out_specs=P(("groups", "row"), "col", None),
        check_vma=False,
    )
```

```python
import jax
import jax.numpy as jnp
from jax import lax
from jax.sharding import PartitionSpec as P

HEADS = 4
G = 8


def with_halo(array, sides, width):
    for axis, dim in sides:
        size, length = (lax.axis_size(axis), array.shape[dim])
        up = [(i, (i + 1) % size) for i in range(size - 1)]
        down = [(j, i) for i, j in up]
        last = lax.slice_in_dim(array, length - width, length, axis=dim)
        initial = lax.slice_in_dim(array, 0, width, axis=dim)
        before = lax.ppermute(last, axis, up)
        after = lax.ppermute(initial, axis, down)
        array = jnp.concatenate([before, array, after], axis=dim)
    return array


def gelu_tanh(values):
    return jax.nn.gelu(values, approximate=True)


def expand_layer(features, expand_weight, expand_bias):
    return gelu_tanh(
        jnp.dot(features, expand_weight, preferred_element_type=jnp.float32) + expand_bias
    ).astype(jnp.bfloat16)


def depthwise(padded, depth_weight, depth_bias, row_count, col_count):
    accumulated = jnp.zeros((row_count, col_count, padded.shape[2]), jnp.float32) + depth_bias
    for row_shift in range(3):
        for col_shift in range(3):
            accumulated = (
                accumulated
                + padded[row_shift : row_shift + row_count, col_shift : col_shift + col_count]
                * depth_weight[row_shift, col_shift]
            )
    return gelu_tanh(accumulated).astype(jnp.bfloat16)


def layer_norm(features, norm_gain, norm_bias):
    values = features.astype(jnp.float32)
    mean_value = jnp.mean(values, axis=-1, keepdims=True)
    variance = jnp.mean((values - mean_value) ** 2, axis=-1, keepdims=True)
    return ((values - mean_value) * lax.rsqrt(variance + 1e-05) * norm_gain + norm_bias).astype(
        jnp.bfloat16
    )


def grid_bias(position_bias, grid_side):
    position = jnp.arange(grid_side * grid_side, dtype=jnp.int32)
    row_of = position // grid_side
    col_of = position % grid_side
    offset_index = (row_of[:, None] - row_of[None, :] + grid_side - 1) * (2 * grid_side - 1) + (
        col_of[:, None] - col_of[None, :] + grid_side - 1
    )
    return jnp.take(position_bias, offset_index, axis=1)


def attend(projected, table, head_count):
    group_count, tokens, triple = projected.shape
    channels = triple // 3
    head_size = channels // head_count
    split_parts = projected.reshape(group_count, tokens, 3, head_count, head_size)
    query_part = split_parts[:, :, 0]
    key_part = split_parts[:, :, 1]
    value_part = split_parts[:, :, 2]
    scores = (
        jnp.einsum("nqhd,nkhd->nhqk", query_part, key_part, preferred_element_type=jnp.float32)
        * head_size ** (-0.5)
        + table[None]
    )
    probs = jax.nn.softmax(scores, axis=-1).astype(jnp.bfloat16)
    attended = jnp.einsum("nhqk,nkhd->nqhd", probs, value_part, preferred_element_type=jnp.float32)
    return attended.astype(jnp.bfloat16).reshape(group_count, tokens, channels)


def body(
    sky_map,
    expand_weight,
    expand_bias,
    depth_weight,
    depth_bias,
    project_weight,
    project_bias,
    norm_gain,
    norm_bias,
    mixing_weight,
    position_bias,
    output_weight,
):
    row_count, col_count, channels = sky_map.shape
    row_size = lax.axis_size("row")
    expanded = expand_layer(sky_map, expand_weight, expand_bias)
    padded = with_halo(expanded, (("row", 0), ("col", 1)), 1)
    across = G // lax.axis_size("col")
    stride = col_count // across
    table = grid_bias(position_bias, G)
    pieces = 2 if row_count % (2 * row_size) == 0 and (row_count // 2) % G == 0 else 1
    span = row_count // pieces
    outs = []
    for piece in range(pieces):
        first = piece * span
        hidden = depthwise(padded[first : first + span + 2], depth_weight, depth_bias, span, col_count)
        after_conv = (
            sky_map[first : first + span].astype(jnp.float32)
            + jnp.dot(hidden, project_weight, preferred_element_type=jnp.float32)
            + project_bias
        ).astype(jnp.bfloat16)
        normed = layer_norm(after_conv, norm_gain, norm_bias)
        moved = lax.all_to_all(
            lax.all_to_all(
                normed.reshape(span, across, stride, channels),
                "row",
                split_axis=0,
                concat_axis=0,
                tiled=True,
            ),
            "col",
            split_axis=2,
            concat_axis=1,
            tiled=True,
        )
        projected = jnp.dot(moved, mixing_weight, preferred_element_type=jnp.float32).astype(
            jnp.bfloat16
        )
        inner_rows = span // G
        inner_cols = projected.shape[2]
        grouped = (
            projected.reshape(G, inner_rows, G, inner_cols, 3 * channels)
            .transpose(1, 3, 0, 2, 4)
            .reshape(inner_rows, inner_cols, G * G, 3 * channels)
        )
        heads_out = lax.map(lambda block: attend(block, table, HEADS), grouped)
        returned = (
            heads_out.reshape(inner_rows, inner_cols, G, G, channels)
            .transpose(2, 0, 3, 1, 4)
            .reshape(span, G, inner_cols, channels)
        )
        returned = lax.all_to_all(
            lax.all_to_all(returned, "row", split_axis=0, concat_axis=0, tiled=True),
            "col",
            split_axis=1,
            concat_axis=2,
            tiled=True,
        )
        returned = returned.reshape(span, col_count, channels)
        outs.append(
            (
                after_conv.astype(jnp.float32)
                + jnp.dot(returned, output_weight, preferred_element_type=jnp.float32)
            ).astype(jnp.bfloat16)
        )
    return jnp.concatenate(outs, axis=0)


def solution(mesh):
    placed = (
        P(("groups", "row"), "col", None),
        P(),
        P(),
        P(),
        P(),
        P(),
        P(),
        P(),
        P(),
        P(),
        P(),
        P(),
    )
    return jax.shard_map(
        body,
        mesh=mesh,
        in_specs=placed,
        out_specs=P(("groups", "row"), "col", None),
        check_vma=False,
    )
```

```python
import jax
import jax.numpy as jnp
from jax import lax
from jax.sharding import PartitionSpec as P

HEADS = 4
G = 8


def with_halo(array, sides, width):
    for axis, dim in sides:
        size, length = (lax.axis_size(axis), array.shape[dim])
        up = [(i, (i + 1) % size) for i in range(size - 1)]
        down = [(j, i) for i, j in up]
        last = lax.slice_in_dim(array, length - width, length, axis=dim)
        initial = lax.slice_in_dim(array, 0, width, axis=dim)
        before = lax.ppermute(last, axis, up)
        after = lax.ppermute(initial, axis, down)
        array = jnp.concatenate([before, array, after], axis=dim)
    return array


def gelu_tanh(values):
    return jax.nn.gelu(values, approximate=True)


def expand_layer(features, expand_weight, expand_bias):
    return gelu_tanh(
        jnp.dot(features, expand_weight, preferred_element_type=jnp.float32) + expand_bias
    ).astype(jnp.bfloat16)


def depthwise(padded, depth_weight, depth_bias, row_count, col_count):
    accumulated = jnp.zeros((row_count, col_count, padded.shape[2]), jnp.float32) + depth_bias
    for row_shift in range(3):
        for col_shift in range(3):
            accumulated = (
                accumulated
                + padded[row_shift : row_shift + row_count, col_shift : col_shift + col_count]
                * depth_weight[row_shift, col_shift]
            )
    return gelu_tanh(accumulated).astype(jnp.bfloat16)


def layer_norm(features, norm_gain, norm_bias):
    values = features.astype(jnp.float32)
    mean_value = jnp.mean(values, axis=-1, keepdims=True)
    variance = jnp.mean((values - mean_value) ** 2, axis=-1, keepdims=True)
    return ((values - mean_value) * lax.rsqrt(variance + 1e-05) * norm_gain + norm_bias).astype(
        jnp.bfloat16
    )


def grid_bias(position_bias, grid_side):
    position = jnp.arange(grid_side * grid_side, dtype=jnp.int32)
    row_of = position // grid_side
    col_of = position % grid_side
    offset_index = (row_of[:, None] - row_of[None, :] + grid_side - 1) * (2 * grid_side - 1) + (
        col_of[:, None] - col_of[None, :] + grid_side - 1
    )
    return jnp.take(position_bias, offset_index, axis=1)


def attend(projected, table, head_count):
    group_count, tokens, triple = projected.shape
    channels = triple // 3
    head_size = channels // head_count
    split_parts = projected.reshape(group_count, tokens, 3, head_count, head_size)
    query_part = split_parts[:, :, 0]
    key_part = split_parts[:, :, 1]
    value_part = split_parts[:, :, 2]
    scores = (
        jnp.einsum("nqhd,nkhd->nhqk", query_part, key_part, preferred_element_type=jnp.float32)
        * head_size ** (-0.5)
        + table[None]
    )
    probs = jax.nn.softmax(scores, axis=-1).astype(jnp.bfloat16)
    attended = jnp.einsum("nhqk,nkhd->nqhd", probs, value_part, preferred_element_type=jnp.float32)
    return attended.astype(jnp.bfloat16).reshape(group_count, tokens, channels)


def body(
    sky_map,
    expand_weight,
    expand_bias,
    depth_weight,
    depth_bias,
    project_weight,
    project_bias,
    norm_gain,
    norm_bias,
    mixing_weight,
    position_bias,
    output_weight,
):
    row_count, col_count, channels = sky_map.shape
    row_size = lax.axis_size("row")
    expanded = expand_layer(sky_map, expand_weight, expand_bias)
    padded = with_halo(expanded, (("row", 0), ("col", 1)), 1)
    across = G // lax.axis_size("col")
    stride = col_count // across
    table = grid_bias(position_bias, G)
    pieces = next(n for n in (4, 2, 1) if row_count % (n * row_size) == 0 and (row_count // n) % G == 0)
    span = row_count // pieces
    outs = []
    for piece in range(pieces):
        first = piece * span
        hidden = depthwise(padded[first : first + span + 2], depth_weight, depth_bias, span, col_count)
        after_conv = (
            sky_map[first : first + span].astype(jnp.float32)
            + jnp.dot(hidden, project_weight, preferred_element_type=jnp.float32)
            + project_bias
        ).astype(jnp.bfloat16)
        normed = layer_norm(after_conv, norm_gain, norm_bias)
        moved = lax.all_to_all(
            lax.all_to_all(
                normed.reshape(span, across, stride, channels),
                "row",
                split_axis=0,
                concat_axis=0,
                tiled=True,
            ),
            "col",
            split_axis=2,
            concat_axis=1,
            tiled=True,
        )
        projected = jnp.dot(moved, mixing_weight, preferred_element_type=jnp.float32).astype(
            jnp.bfloat16
        )
        inner_rows = span // G
        inner_cols = projected.shape[2]
        grouped = (
            projected.reshape(G, inner_rows, G, inner_cols, 3 * channels)
            .transpose(1, 3, 0, 2, 4)
            .reshape(inner_rows, inner_cols, G * G, 3 * channels)
        )
        heads_out = lax.map(lambda block: attend(block, table, HEADS), grouped)
        returned = (
            heads_out.reshape(inner_rows, inner_cols, G, G, channels)
            .transpose(2, 0, 3, 1, 4)
            .reshape(span, G, inner_cols, channels)
        )
        returned = lax.all_to_all(
            lax.all_to_all(returned, "row", split_axis=0, concat_axis=0, tiled=True),
            "col",
            split_axis=1,
            concat_axis=2,
            tiled=True,
        )
        returned = returned.reshape(span, col_count, channels)
        outs.append(
            (
                after_conv.astype(jnp.float32)
                + jnp.dot(returned, output_weight, preferred_element_type=jnp.float32)
            ).astype(jnp.bfloat16)
        )
    return jnp.concatenate(outs, axis=0)


def solution(mesh):
    placed = (
        P(("groups", "row"), "col", None),
        P(),
        P(),
        P(),
        P(),
        P(),
        P(),
        P(),
        P(),
        P(),
        P(),
        P(),
    )
    return jax.shard_map(
        body,
        mesh=mesh,
        in_specs=placed,
        out_specs=P(("groups", "row"), "col", None),
        check_vma=False,
    )
```

```python
import jax
import jax.numpy as jnp
from jax import lax
from jax.sharding import PartitionSpec as P
from jax.experimental import pallas as pl

HEADS = 4
G = 8


def with_halo(array, sides, width):
    for axis, dim in sides:
        size, length = (lax.axis_size(axis), array.shape[dim])
        up = [(i, (i + 1) % size) for i in range(size - 1)]
        down = [(j, i) for i, j in up]
        last = lax.slice_in_dim(array, length - width, length, axis=dim)
        initial = lax.slice_in_dim(array, 0, width, axis=dim)
        before = lax.ppermute(last, axis, up)
        after = lax.ppermute(initial, axis, down)
        array = jnp.concatenate([before, array, after], axis=dim)
    return array


def gelu_tanh(values):
    return jax.nn.gelu(values, approximate=True)


def expand_layer(features, expand_weight, expand_bias):
    return gelu_tanh(
        jnp.dot(features, expand_weight, preferred_element_type=jnp.float32) + expand_bias
    ).astype(jnp.bfloat16)


def depthwise(padded, depth_weight, depth_bias, row_count, col_count):
    accumulated = jnp.zeros((row_count, col_count, padded.shape[2]), jnp.float32) + depth_bias
    for row_shift in range(3):
        for col_shift in range(3):
            accumulated = (
                accumulated
                + padded[row_shift : row_shift + row_count, col_shift : col_shift + col_count]
                * depth_weight[row_shift, col_shift]
            )
    return gelu_tanh(accumulated).astype(jnp.bfloat16)


def layer_norm(features, norm_gain, norm_bias):
    values = features.astype(jnp.float32)
    mean_value = jnp.mean(values, axis=-1, keepdims=True)
    variance = jnp.mean((values - mean_value) ** 2, axis=-1, keepdims=True)
    return ((values - mean_value) * lax.rsqrt(variance + 1e-05) * norm_gain + norm_bias).astype(
        jnp.bfloat16
    )


def grid_bias(position_bias, grid_side):
    position = jnp.arange(grid_side * grid_side, dtype=jnp.int32)
    row_of = position // grid_side
    col_of = position % grid_side
    offset_index = (row_of[:, None] - row_of[None, :] + grid_side - 1) * (2 * grid_side - 1) + (
        col_of[:, None] - col_of[None, :] + grid_side - 1
    )
    return jnp.take(position_bias, offset_index, axis=1)


def attend(projected, table, head_count):
    group_count, tokens, triple = projected.shape
    channels = triple // 3
    head_size = channels // head_count
    split_parts = projected.reshape(group_count, tokens, 3, head_count, head_size)
    query_part = split_parts[:, :, 0]
    key_part = split_parts[:, :, 1]
    value_part = split_parts[:, :, 2]
    scores = (
        jnp.einsum("nqhd,nkhd->nhqk", query_part, key_part, preferred_element_type=jnp.float32)
        * head_size ** (-0.5)
        + table[None]
    )
    probs = jax.nn.softmax(scores, axis=-1).astype(jnp.bfloat16)
    attended = jnp.einsum("nhqk,nkhd->nqhd", probs, value_part, preferred_element_type=jnp.float32)
    return attended.astype(jnp.bfloat16).reshape(group_count, tokens, channels)


def attention_kernel(x_ref, w_ref, bias_ref, o_ref):
    block, tokens, channels = x_ref.shape
    head_size = channels // HEADS
    x = x_ref[...].reshape(block * tokens, channels)
    qkv = jnp.dot(x, w_ref[...], preferred_element_type=jnp.float32).astype(jnp.bfloat16)
    query = qkv[:, :channels]
    key = qkv[:, channels : 2 * channels].reshape(block, tokens, channels)
    value = qkv[:, 2 * channels :]
    head_of = lax.broadcasted_iota(jnp.int32, (1, channels), 1) // head_size
    out = jnp.zeros((block, tokens, channels), jnp.float32)
    for head in range(HEADS):
        mask = head_of == head
        masked_query = jnp.where(mask, query, jnp.zeros_like(query)).reshape(block, tokens, channels)
        scores = (
            jnp.einsum("gtd,gud->gtu", masked_query, key, preferred_element_type=jnp.float32)
            * head_size ** (-0.5)
            + bias_ref[head][None]
        )
        shifted = jnp.exp(scores - jnp.max(scores, axis=-1, keepdims=True))
        probs = (shifted / jnp.sum(shifted, axis=-1, keepdims=True)).astype(jnp.bfloat16)
        masked_value = jnp.where(mask, value, jnp.zeros_like(value)).reshape(block, tokens, channels)
        part = jnp.einsum("gtu,gud->gtd", probs, masked_value, preferred_element_type=jnp.float32)
        out = jnp.where(mask.reshape(1, 1, channels), part, out)
    o_ref[...] = out.astype(o_ref.dtype)


def grid_attention(grouped, mixing_weight, table):
    count, tokens, channels = grouped.shape
    block = next(b for b in (32, 16, 8, 4, 2, 1) if count % b == 0)
    return pl.pallas_call(
        attention_kernel,
        grid=(count // block,),
        in_specs=[
            pl.BlockSpec((block, tokens, channels), lambda i: (i, 0, 0)),
            pl.BlockSpec(mixing_weight.shape, lambda i: (0, 0)),
            pl.BlockSpec(table.shape, lambda i: (0, 0, 0)),
        ],
        out_specs=pl.BlockSpec((block, tokens, channels), lambda i: (i, 0, 0)),
        out_shape=jax.ShapeDtypeStruct((count, tokens, channels), jnp.bfloat16),
    )(grouped, mixing_weight, table)


def body(
    sky_map,
    expand_weight,
    expand_bias,
    depth_weight,
    depth_bias,
    project_weight,
    project_bias,
    norm_gain,
    norm_bias,
    mixing_weight,
    position_bias,
    output_weight,
):
    row_count, col_count, channels = sky_map.shape
    row_size = lax.axis_size("row")
    expanded = expand_layer(sky_map, expand_weight, expand_bias)
    padded = with_halo(expanded, (("row", 0), ("col", 1)), 1)
    across = G // lax.axis_size("col")
    stride = col_count // across
    table = grid_bias(position_bias, G)
    pieces = 2 if row_count % (2 * row_size) == 0 and (row_count // 2) % G == 0 else 1
    span = row_count // pieces
    outs = []
    for piece in range(pieces):
        first = piece * span
        hidden = depthwise(padded[first : first + span + 2], depth_weight, depth_bias, span, col_count)
        after_conv = (
            sky_map[first : first + span].astype(jnp.float32)
            + jnp.dot(hidden, project_weight, preferred_element_type=jnp.float32)
            + project_bias
        ).astype(jnp.bfloat16)
        normed = layer_norm(after_conv, norm_gain, norm_bias)
        moved = lax.all_to_all(
            lax.all_to_all(
                normed.reshape(span, across, stride, channels),
                "row",
                split_axis=0,
                concat_axis=0,
                tiled=True,
            ),
            "col",
            split_axis=2,
            concat_axis=1,
            tiled=True,
        )
        inner_rows = span // G
        inner_cols = moved.shape[2]
        grouped = (
            moved.reshape(G, inner_rows, G, inner_cols, channels)
            .transpose(1, 3, 0, 2, 4)
            .reshape(inner_rows * inner_cols, G * G, channels)
        )
        heads_out = grid_attention(grouped, mixing_weight, table)
        returned = (
            heads_out.reshape(inner_rows, inner_cols, G, G, channels)
            .transpose(2, 0, 3, 1, 4)
            .reshape(span, G, inner_cols, channels)
        )
        returned = lax.all_to_all(
            lax.all_to_all(returned, "row", split_axis=0, concat_axis=0, tiled=True),
            "col",
            split_axis=1,
            concat_axis=2,
            tiled=True,
        )
        returned = returned.reshape(span, col_count, channels)
        outs.append(
            (
                after_conv.astype(jnp.float32)
                + jnp.dot(returned, output_weight, preferred_element_type=jnp.float32)
            ).astype(jnp.bfloat16)
        )
    return jnp.concatenate(outs, axis=0)


def solution(mesh):
    placed = (
        P(("groups", "row"), "col", None),
        P(),
        P(),
        P(),
        P(),
        P(),
        P(),
        P(),
        P(),
        P(),
        P(),
        P(),
    )
    return jax.shard_map(
        body,
        mesh=mesh,
        in_specs=placed,
        out_specs=P(("groups", "row"), "col", None),
        check_vma=False,
    )
```

```python
import jax
import jax.numpy as jnp
from jax import lax
from jax.sharding import PartitionSpec as P
from jax.experimental import pallas as pl

HEADS = 4
G = 8


def with_halo(array, sides, width):
    for axis, dim in sides:
        size, length = (lax.axis_size(axis), array.shape[dim])
        up = [(i, (i + 1) % size) for i in range(size - 1)]
        down = [(j, i) for i, j in up]
        last = lax.slice_in_dim(array, length - width, length, axis=dim)
        initial = lax.slice_in_dim(array, 0, width, axis=dim)
        before = lax.ppermute(last, axis, up)
        after = lax.ppermute(initial, axis, down)
        array = jnp.concatenate([before, array, after], axis=dim)
    return array


def gelu_tanh(values):
    return jax.nn.gelu(values, approximate=True)


def expand_layer(features, expand_weight, expand_bias):
    return gelu_tanh(
        jnp.dot(features, expand_weight, preferred_element_type=jnp.float32) + expand_bias
    ).astype(jnp.bfloat16)


def depthwise(padded, depth_weight, depth_bias, row_count, col_count):
    accumulated = jnp.zeros((row_count, col_count, padded.shape[2]), jnp.float32) + depth_bias
    for row_shift in range(3):
        for col_shift in range(3):
            accumulated = (
                accumulated
                + padded[row_shift : row_shift + row_count, col_shift : col_shift + col_count]
                * depth_weight[row_shift, col_shift]
            )
    return gelu_tanh(accumulated).astype(jnp.bfloat16)


def layer_norm(features, norm_gain, norm_bias):
    values = features.astype(jnp.float32)
    mean_value = jnp.mean(values, axis=-1, keepdims=True)
    variance = jnp.mean((values - mean_value) ** 2, axis=-1, keepdims=True)
    return ((values - mean_value) * lax.rsqrt(variance + 1e-05) * norm_gain + norm_bias).astype(
        jnp.bfloat16
    )


def grid_bias(position_bias, grid_side):
    position = jnp.arange(grid_side * grid_side, dtype=jnp.int32)
    row_of = position // grid_side
    col_of = position % grid_side
    offset_index = (row_of[:, None] - row_of[None, :] + grid_side - 1) * (2 * grid_side - 1) + (
        col_of[:, None] - col_of[None, :] + grid_side - 1
    )
    return jnp.take(position_bias, offset_index, axis=1)


def attend(projected, table, head_count):
    group_count, tokens, triple = projected.shape
    channels = triple // 3
    head_size = channels // head_count
    split_parts = projected.reshape(group_count, tokens, 3, head_count, head_size)
    query_part = split_parts[:, :, 0]
    key_part = split_parts[:, :, 1]
    value_part = split_parts[:, :, 2]
    scores = (
        jnp.einsum("nqhd,nkhd->nhqk", query_part, key_part, preferred_element_type=jnp.float32)
        * head_size ** (-0.5)
        + table[None]
    )
    probs = jax.nn.softmax(scores, axis=-1).astype(jnp.bfloat16)
    attended = jnp.einsum("nhqk,nkhd->nqhd", probs, value_part, preferred_element_type=jnp.float32)
    return attended.astype(jnp.bfloat16).reshape(group_count, tokens, channels)


def attention_kernel(x_ref, w_ref, bias_ref, o_ref):
    block, tokens, channels = x_ref.shape
    head_size = channels // HEADS
    x = x_ref[...].reshape(block * tokens, channels)
    qkv = jnp.dot(x, w_ref[...], preferred_element_type=jnp.float32).astype(jnp.bfloat16)
    query = qkv[:, :channels]
    key = qkv[:, channels : 2 * channels].reshape(block, tokens, channels)
    value = qkv[:, 2 * channels :]
    head_of = lax.broadcasted_iota(jnp.int32, (1, channels), 1) // head_size
    out = jnp.zeros((block, tokens, channels), jnp.float32)
    for head in range(HEADS):
        mask = head_of == head
        masked_query = jnp.where(mask, query, jnp.zeros_like(query)).reshape(block, tokens, channels)
        scores = (
            jnp.einsum("gtd,gud->gtu", masked_query, key, preferred_element_type=jnp.float32)
            * head_size ** (-0.5)
            + bias_ref[head][None]
        )
        shifted = jnp.exp(scores - jnp.max(scores, axis=-1, keepdims=True))
        probs = (shifted / jnp.sum(shifted, axis=-1, keepdims=True)).astype(jnp.bfloat16)
        masked_value = jnp.where(mask, value, jnp.zeros_like(value)).reshape(block, tokens, channels)
        part = jnp.einsum("gtu,gud->gtd", probs, masked_value, preferred_element_type=jnp.float32)
        out = jnp.where(mask.reshape(1, 1, channels), part, out)
    o_ref[...] = out.astype(o_ref.dtype)


def grid_attention(grouped, mixing_weight, table):
    count, tokens, channels = grouped.shape
    block = next(b for b in (32, 16, 8, 4, 2, 1) if count % b == 0)
    return pl.pallas_call(
        attention_kernel,
        grid=(count // block,),
        in_specs=[
            pl.BlockSpec((block, tokens, channels), lambda i: (i, 0, 0)),
            pl.BlockSpec(mixing_weight.shape, lambda i: (0, 0)),
            pl.BlockSpec(table.shape, lambda i: (0, 0, 0)),
        ],
        out_specs=pl.BlockSpec((block, tokens, channels), lambda i: (i, 0, 0)),
        out_shape=jax.ShapeDtypeStruct((count, tokens, channels), jnp.bfloat16),
    )(grouped, mixing_weight, table)


def pieces_of(normed, row_size, col_size, pp, span, col_count, channels):
    across = G // col_size
    inner_cols = col_count // across // col_size
    return (
        normed.reshape(row_size, pp, across, col_size, inner_cols, channels)
        .transpose(0, 3, 1, 2, 4, 5)
        .reshape(row_size * col_size, pp, across, inner_cols, channels)
    )


def body(
    sky_map,
    expand_weight,
    expand_bias,
    depth_weight,
    depth_bias,
    project_weight,
    project_bias,
    norm_gain,
    norm_bias,
    mixing_weight,
    position_bias,
    output_weight,
):
    row_count, col_count, channels = sky_map.shape
    row_size = lax.axis_size("row")
    expanded = expand_layer(sky_map, expand_weight, expand_bias)
    padded = with_halo(expanded, (("row", 0), ("col", 1)), 1)
    across = G // lax.axis_size("col")
    stride = col_count // across
    table = grid_bias(position_bias, G)
    pieces = 2 if row_count % (2 * row_size) == 0 and (row_count // 2) % G == 0 else 1
    span = row_count // pieces
    col_size = lax.axis_size("col")
    sub = row_size // G
    pp = span // row_size
    inner_cols = stride // col_size
    outs = []
    for piece in range(pieces):
        first = piece * span
        hidden = depthwise(padded[first : first + span + 2], depth_weight, depth_bias, span, col_count)
        after_conv = (
            sky_map[first : first + span].astype(jnp.float32)
            + jnp.dot(hidden, project_weight, preferred_element_type=jnp.float32)
            + project_bias
        ).astype(jnp.bfloat16)
        normed = layer_norm(after_conv, norm_gain, norm_bias)
        pair = pieces_of(normed, row_size, col_size, pp, span, col_count, channels)
        moved = lax.all_to_all(pair, ("row", "col"), 0, 0, tiled=True)
        grouped = (
            moved.reshape(G, sub, col_size, pp, across, inner_cols, channels)
            .transpose(1, 3, 5, 0, 2, 4, 6)
            .reshape(sub * pp * inner_cols, G * G, channels)
        )
        heads_out = grid_attention(grouped, mixing_weight, table)
        returned = (
            heads_out.reshape(sub, pp, inner_cols, G, col_size, across, channels)
            .transpose(3, 0, 4, 1, 5, 2, 6)
            .reshape(row_size * col_size, pp, across, inner_cols, channels)
        )
        returned = lax.all_to_all(returned, ("row", "col"), 0, 0, tiled=True)
        returned = (
            returned.reshape(row_size, col_size, pp, across, inner_cols, channels)
            .transpose(0, 2, 3, 1, 4, 5)
            .reshape(span, col_count, channels)
        )
        outs.append(
            (
                after_conv.astype(jnp.float32)
                + jnp.dot(returned, output_weight, preferred_element_type=jnp.float32)
            ).astype(jnp.bfloat16)
        )
    return jnp.concatenate(outs, axis=0)


def solution(mesh):
    placed = (
        P(("groups", "row"), "col", None),
        P(),
        P(),
        P(),
        P(),
        P(),
        P(),
        P(),
        P(),
        P(),
        P(),
        P(),
    )
    return jax.shard_map(
        body,
        mesh=mesh,
        in_specs=placed,
        out_specs=P(("groups", "row"), "col", None),
        check_vma=False,
    )
```

```python
import jax
import jax.numpy as jnp
from jax import lax
from jax.sharding import PartitionSpec as P
from jax.experimental import pallas as pl

HEADS = 4
G = 8


def with_halo(array, sides, width):
    for axis, dim in sides:
        size, length = (lax.axis_size(axis), array.shape[dim])
        up = [(i, (i + 1) % size) for i in range(size - 1)]
        down = [(j, i) for i, j in up]
        last = lax.slice_in_dim(array, length - width, length, axis=dim)
        initial = lax.slice_in_dim(array, 0, width, axis=dim)
        before = lax.ppermute(last, axis, up)
        after = lax.ppermute(initial, axis, down)
        array = jnp.concatenate([before, array, after], axis=dim)
    return array


def gelu_tanh(values):
    return jax.nn.gelu(values, approximate=True)


def expand_layer(features, expand_weight, expand_bias):
    return gelu_tanh(
        jnp.dot(features, expand_weight, preferred_element_type=jnp.float32) + expand_bias
    ).astype(jnp.bfloat16)


def depthwise(padded, depth_weight, depth_bias, row_count, col_count):
    accumulated = jnp.zeros((row_count, col_count, padded.shape[2]), jnp.float32) + depth_bias
    for row_shift in range(3):
        for col_shift in range(3):
            accumulated = (
                accumulated
                + padded[row_shift : row_shift + row_count, col_shift : col_shift + col_count]
                * depth_weight[row_shift, col_shift]
            )
    return gelu_tanh(accumulated).astype(jnp.bfloat16)


def layer_norm(features, norm_gain, norm_bias):
    values = features.astype(jnp.float32)
    mean_value = jnp.mean(values, axis=-1, keepdims=True)
    variance = jnp.mean((values - mean_value) ** 2, axis=-1, keepdims=True)
    return ((values - mean_value) * lax.rsqrt(variance + 1e-05) * norm_gain + norm_bias).astype(
        jnp.bfloat16
    )


def grid_bias(position_bias, grid_side):
    position = jnp.arange(grid_side * grid_side, dtype=jnp.int32)
    row_of = position // grid_side
    col_of = position % grid_side
    offset_index = (row_of[:, None] - row_of[None, :] + grid_side - 1) * (2 * grid_side - 1) + (
        col_of[:, None] - col_of[None, :] + grid_side - 1
    )
    return jnp.take(position_bias, offset_index, axis=1)


def attend(projected, table, head_count):
    group_count, tokens, triple = projected.shape
    channels = triple // 3
    head_size = channels // head_count
    split_parts = projected.reshape(group_count, tokens, 3, head_count, head_size)
    query_part = split_parts[:, :, 0]
    key_part = split_parts[:, :, 1]
    value_part = split_parts[:, :, 2]
    scores = (
        jnp.einsum("nqhd,nkhd->nhqk", query_part, key_part, preferred_element_type=jnp.float32)
        * head_size ** (-0.5)
        + table[None]
    )
    probs = jax.nn.softmax(scores, axis=-1).astype(jnp.bfloat16)
    attended = jnp.einsum("nhqk,nkhd->nqhd", probs, value_part, preferred_element_type=jnp.float32)
    return attended.astype(jnp.bfloat16).reshape(group_count, tokens, channels)


def attention_kernel(x_ref, w_ref, bias_ref, o_ref):
    block, tokens, channels = x_ref.shape
    head_size = channels // HEADS
    x = x_ref[...].reshape(block * tokens, channels)
    qkv = jnp.dot(x, w_ref[...], preferred_element_type=jnp.float32).astype(jnp.bfloat16)
    query = qkv[:, :channels]
    key = qkv[:, channels : 2 * channels].reshape(block, tokens, channels)
    value = qkv[:, 2 * channels :]
    head_of = lax.broadcasted_iota(jnp.int32, (1, channels), 1) // head_size
    out = jnp.zeros((block, tokens, channels), jnp.float32)
    for head in range(HEADS):
        mask = head_of == head
        masked_query = jnp.where(mask, query, jnp.zeros_like(query)).reshape(block, tokens, channels)
        scores = (
            jnp.einsum("gtd,gud->gtu", masked_query, key, preferred_element_type=jnp.float32)
            * head_size ** (-0.5)
            + bias_ref[head][None]
        )
        shifted = jnp.exp(scores - jnp.max(scores, axis=-1, keepdims=True))
        probs = (shifted / jnp.sum(shifted, axis=-1, keepdims=True)).astype(jnp.bfloat16)
        masked_value = jnp.where(mask, value, jnp.zeros_like(value)).reshape(block, tokens, channels)
        part = jnp.einsum("gtu,gud->gtd", probs, masked_value, preferred_element_type=jnp.float32)
        out = jnp.where(mask.reshape(1, 1, channels), part, out)
    o_ref[...] = out.astype(o_ref.dtype)


def grid_attention(grouped, mixing_weight, table):
    count, tokens, channels = grouped.shape
    block = next(b for b in (32, 16, 8, 4, 2, 1) if count % b == 0)
    return pl.pallas_call(
        attention_kernel,
        grid=(count // block,),
        in_specs=[
            pl.BlockSpec((block, tokens, channels), lambda i: (i, 0, 0)),
            pl.BlockSpec(mixing_weight.shape, lambda i: (0, 0)),
            pl.BlockSpec(table.shape, lambda i: (0, 0, 0)),
        ],
        out_specs=pl.BlockSpec((block, tokens, channels), lambda i: (i, 0, 0)),
        out_shape=jax.ShapeDtypeStruct((count, tokens, channels), jnp.bfloat16),
    )(grouped, mixing_weight, table)


def pieces_of(normed, row_size, col_size, pp, span, col_count, channels):
    across = G // col_size
    inner_cols = col_count // across // col_size
    return (
        normed.reshape(row_size, pp, across, col_size, inner_cols, channels)
        .transpose(0, 3, 1, 2, 4, 5)
        .reshape(row_size * col_size, pp, across, inner_cols, channels)
    )


def body(
    sky_map,
    expand_weight,
    expand_bias,
    depth_weight,
    depth_bias,
    project_weight,
    project_bias,
    norm_gain,
    norm_bias,
    mixing_weight,
    position_bias,
    output_weight,
):
    row_count, col_count, channels = sky_map.shape
    row_size = lax.axis_size("row")
    expanded = expand_layer(sky_map, expand_weight, expand_bias)
    padded = with_halo(expanded, (("row", 0), ("col", 1)), 1)
    across = G // lax.axis_size("col")
    stride = col_count // across
    table = grid_bias(position_bias, G)
    pieces = 2 if row_count % (2 * row_size) == 0 and (row_count // 2) % G == 0 else 1
    span = row_count // pieces
    col_size = lax.axis_size("col")
    sub = row_size // G
    pp = span // row_size
    inner_cols = stride // col_size
    outs = []
    for piece in range(pieces):
        first = piece * span
        hidden = depthwise(padded[first : first + span + 2], depth_weight, depth_bias, span, col_count)
        after_conv = (
            sky_map[first : first + span].astype(jnp.float32)
            + jnp.dot(hidden, project_weight, preferred_element_type=jnp.float32)
            + project_bias
        ).astype(jnp.bfloat16)
        normed = layer_norm(after_conv, norm_gain, norm_bias)
        pair = pieces_of(normed, row_size, col_size, pp, span, col_count, channels)
        if piece + 1 < pieces:
            pair, padded = lax.optimization_barrier((pair, padded))
        moved = lax.all_to_all(pair, ("row", "col"), 0, 0, tiled=True)
        grouped = (
            moved.reshape(G, sub, col_size, pp, across, inner_cols, channels)
            .transpose(1, 3, 5, 0, 2, 4, 6)
            .reshape(sub * pp * inner_cols, G * G, channels)
        )
        heads_out = grid_attention(grouped, mixing_weight, table)
        returned = (
            heads_out.reshape(sub, pp, inner_cols, G, col_size, across, channels)
            .transpose(3, 0, 4, 1, 5, 2, 6)
            .reshape(row_size * col_size, pp, across, inner_cols, channels)
        )
        returned = lax.all_to_all(returned, ("row", "col"), 0, 0, tiled=True)
        returned = (
            returned.reshape(row_size, col_size, pp, across, inner_cols, channels)
            .transpose(0, 2, 3, 1, 4, 5)
            .reshape(span, col_count, channels)
        )
        outs.append(
            (
                after_conv.astype(jnp.float32)
                + jnp.dot(returned, output_weight, preferred_element_type=jnp.float32)
            ).astype(jnp.bfloat16)
        )
    return jnp.concatenate(outs, axis=0)


def solution(mesh):
    placed = (
        P(("groups", "row"), "col", None),
        P(),
        P(),
        P(),
        P(),
        P(),
        P(),
        P(),
        P(),
        P(),
        P(),
        P(),
    )
    return jax.shard_map(
        body,
        mesh=mesh,
        in_specs=placed,
        out_specs=P(("groups", "row"), "col", None),
        check_vma=False,
    )
```

```python
import jax
import jax.numpy as jnp
from jax import lax
from jax.sharding import PartitionSpec as P
from jax.experimental import pallas as pl

HEADS = 4
G = 8


def with_halo(array, sides, width):
    for axis, dim in sides:
        size, length = (lax.axis_size(axis), array.shape[dim])
        up = [(i, (i + 1) % size) for i in range(size - 1)]
        down = [(j, i) for i, j in up]
        last = lax.slice_in_dim(array, length - width, length, axis=dim)
        initial = lax.slice_in_dim(array, 0, width, axis=dim)
        before = lax.ppermute(last, axis, up)
        after = lax.ppermute(initial, axis, down)
        array = jnp.concatenate([before, array, after], axis=dim)
    return array


def gelu_tanh(values):
    return jax.nn.gelu(values, approximate=True)


def expand_layer(features, expand_weight, expand_bias):
    return gelu_tanh(
        jnp.dot(features, expand_weight, preferred_element_type=jnp.float32) + expand_bias
    ).astype(jnp.bfloat16)


def depthwise(padded, depth_weight, depth_bias, row_count, col_count):
    accumulated = jnp.zeros((row_count, col_count, padded.shape[2]), jnp.float32) + depth_bias
    for row_shift in range(3):
        for col_shift in range(3):
            accumulated = (
                accumulated
                + padded[row_shift : row_shift + row_count, col_shift : col_shift + col_count]
                * depth_weight[row_shift, col_shift]
            )
    return gelu_tanh(accumulated).astype(jnp.bfloat16)


def layer_norm(features, norm_gain, norm_bias):
    values = features.astype(jnp.float32)
    mean_value = jnp.mean(values, axis=-1, keepdims=True)
    variance = jnp.mean((values - mean_value) ** 2, axis=-1, keepdims=True)
    return ((values - mean_value) * lax.rsqrt(variance + 1e-05) * norm_gain + norm_bias).astype(
        jnp.bfloat16
    )


def grid_bias(position_bias, grid_side):
    position = jnp.arange(grid_side * grid_side, dtype=jnp.int32)
    row_of = position // grid_side
    col_of = position % grid_side
    offset_index = (row_of[:, None] - row_of[None, :] + grid_side - 1) * (2 * grid_side - 1) + (
        col_of[:, None] - col_of[None, :] + grid_side - 1
    )
    return jnp.take(position_bias, offset_index, axis=1)


def attend(projected, table, head_count):
    group_count, tokens, triple = projected.shape
    channels = triple // 3
    head_size = channels // head_count
    split_parts = projected.reshape(group_count, tokens, 3, head_count, head_size)
    query_part = split_parts[:, :, 0]
    key_part = split_parts[:, :, 1]
    value_part = split_parts[:, :, 2]
    scores = (
        jnp.einsum("nqhd,nkhd->nhqk", query_part, key_part, preferred_element_type=jnp.float32)
        * head_size ** (-0.5)
        + table[None]
    )
    probs = jax.nn.softmax(scores, axis=-1).astype(jnp.bfloat16)
    attended = jnp.einsum("nhqk,nkhd->nqhd", probs, value_part, preferred_element_type=jnp.float32)
    return attended.astype(jnp.bfloat16).reshape(group_count, tokens, channels)


def attention_kernel(x_ref, w_ref, bias_ref, o_ref):
    block, tokens, channels = x_ref.shape
    head_size = channels // HEADS
    x = x_ref[...].reshape(block * tokens, channels)
    qkv = jnp.dot(x, w_ref[...], preferred_element_type=jnp.float32).astype(jnp.bfloat16)
    query = qkv[:, :channels]
    key = qkv[:, channels : 2 * channels].reshape(block, tokens, channels)
    value = qkv[:, 2 * channels :]
    head_of = lax.broadcasted_iota(jnp.int32, (1, channels), 1) // head_size
    out = jnp.zeros((block, tokens, channels), jnp.float32)
    for head in range(HEADS):
        mask = head_of == head
        masked_query = jnp.where(mask, query, jnp.zeros_like(query)).reshape(block, tokens, channels)
        scores = (
            jnp.einsum("gtd,gud->gtu", masked_query, key, preferred_element_type=jnp.float32)
            * head_size ** (-0.5)
            + bias_ref[head][None]
        )
        shifted = jnp.exp(scores - jnp.max(scores, axis=-1, keepdims=True))
        probs = (shifted / jnp.sum(shifted, axis=-1, keepdims=True)).astype(jnp.bfloat16)
        masked_value = jnp.where(mask, value, jnp.zeros_like(value)).reshape(block, tokens, channels)
        part = jnp.einsum("gtu,gud->gtd", probs, masked_value, preferred_element_type=jnp.float32)
        out = jnp.where(mask.reshape(1, 1, channels), part, out)
    o_ref[...] = out.astype(o_ref.dtype)


def grid_attention(grouped, mixing_weight, table):
    count, tokens, channels = grouped.shape
    block = next(b for b in (32, 16, 8, 4, 2, 1) if count % b == 0)
    return pl.pallas_call(
        attention_kernel,
        grid=(count // block,),
        in_specs=[
            pl.BlockSpec((block, tokens, channels), lambda i: (i, 0, 0)),
            pl.BlockSpec(mixing_weight.shape, lambda i: (0, 0)),
            pl.BlockSpec(table.shape, lambda i: (0, 0, 0)),
        ],
        out_specs=pl.BlockSpec((block, tokens, channels), lambda i: (i, 0, 0)),
        out_shape=jax.ShapeDtypeStruct((count, tokens, channels), jnp.bfloat16),
    )(grouped, mixing_weight, table)


def pieces_of(normed, row_size, col_size, pp, span, col_count, channels):
    across = G // col_size
    inner_cols = col_count // across // col_size
    return (
        normed.reshape(row_size, pp, across, col_size, inner_cols, channels)
        .transpose(0, 3, 1, 2, 4, 5)
        .reshape(row_size * col_size, pp, across, inner_cols, channels)
    )


def body(
    sky_map,
    expand_weight,
    expand_bias,
    depth_weight,
    depth_bias,
    project_weight,
    project_bias,
    norm_gain,
    norm_bias,
    mixing_weight,
    position_bias,
    output_weight,
):
    row_count, col_count, channels = sky_map.shape
    row_size = lax.axis_size("row")
    expanded = expand_layer(sky_map, expand_weight, expand_bias)
    padded = with_halo(expanded, (("row", 0), ("col", 1)), 1)
    across = G // lax.axis_size("col")
    stride = col_count // across
    table = grid_bias(position_bias, G)
    pieces = 2 if row_count % (2 * row_size) == 0 and (row_count // 2) % G == 0 else 1
    span = row_count // pieces
    col_size = lax.axis_size("col")
    sub = row_size // G
    pp = span // row_size
    inner_cols = stride // col_size
    windows = [padded[piece * span : piece * span + span + 2] for piece in range(pieces)]
    outs = []
    for piece in range(pieces):
        first = piece * span
        hidden = depthwise(windows[piece], depth_weight, depth_bias, span, col_count)
        after_conv = (
            sky_map[first : first + span].astype(jnp.float32)
            + jnp.dot(hidden, project_weight, preferred_element_type=jnp.float32)
            + project_bias
        ).astype(jnp.bfloat16)
        normed = layer_norm(after_conv, norm_gain, norm_bias)
        pair = pieces_of(normed, row_size, col_size, pp, span, col_count, channels)
        if piece + 1 < pieces:
            pair, windows[piece + 1] = lax.optimization_barrier((pair, windows[piece + 1]))
        moved = lax.all_to_all(pair, ("row", "col"), 0, 0, tiled=True)
        grouped = (
            moved.reshape(G, sub, col_size, pp, across, inner_cols, channels)
            .transpose(1, 3, 5, 0, 2, 4, 6)
            .reshape(sub * pp * inner_cols, G * G, channels)
        )
        heads_out = grid_attention(grouped, mixing_weight, table)
        returned = (
            heads_out.reshape(sub, pp, inner_cols, G, col_size, across, channels)
            .transpose(3, 0, 4, 1, 5, 2, 6)
            .reshape(row_size * col_size, pp, across, inner_cols, channels)
        )
        returned = lax.all_to_all(returned, ("row", "col"), 0, 0, tiled=True)
        returned = (
            returned.reshape(row_size, col_size, pp, across, inner_cols, channels)
            .transpose(0, 2, 3, 1, 4, 5)
            .reshape(span, col_count, channels)
        )
        outs.append(
            (
                after_conv.astype(jnp.float32)
                + jnp.dot(returned, output_weight, preferred_element_type=jnp.float32)
            ).astype(jnp.bfloat16)
        )
    return jnp.concatenate(outs, axis=0)


def solution(mesh):
    placed = (
        P(("groups", "row"), "col", None),
        P(),
        P(),
        P(),
        P(),
        P(),
        P(),
        P(),
        P(),
        P(),
        P(),
        P(),
    )
    return jax.shard_map(
        body,
        mesh=mesh,
        in_specs=placed,
        out_specs=P(("groups", "row"), "col", None),
        check_vma=False,
    )
```

```python
import jax
import jax.numpy as jnp
from jax import lax
from jax.sharding import PartitionSpec as P
from jax.experimental import pallas as pl

HEADS = 4
G = 8


def with_halo(array, sides, width):
    for axis, dim in sides:
        size, length = (lax.axis_size(axis), array.shape[dim])
        up = [(i, (i + 1) % size) for i in range(size - 1)]
        down = [(j, i) for i, j in up]
        last = lax.slice_in_dim(array, length - width, length, axis=dim)
        initial = lax.slice_in_dim(array, 0, width, axis=dim)
        before = lax.ppermute(last, axis, up)
        after = lax.ppermute(initial, axis, down)
        array = jnp.concatenate([before, array, after], axis=dim)
    return array


def gelu_tanh(values):
    return jax.nn.gelu(values, approximate=True)


def expand_layer(features, expand_weight, expand_bias):
    return gelu_tanh(
        jnp.dot(features, expand_weight, preferred_element_type=jnp.float32) + expand_bias
    ).astype(jnp.bfloat16)


def depthwise(padded, depth_weight, depth_bias, row_count, col_count):
    accumulated = jnp.zeros((row_count, col_count, padded.shape[2]), jnp.float32) + depth_bias
    for row_shift in range(3):
        for col_shift in range(3):
            accumulated = (
                accumulated
                + padded[row_shift : row_shift + row_count, col_shift : col_shift + col_count]
                * depth_weight[row_shift, col_shift]
            )
    return gelu_tanh(accumulated).astype(jnp.bfloat16)


def layer_norm(features, norm_gain, norm_bias):
    values = features.astype(jnp.float32)
    mean_value = jnp.mean(values, axis=-1, keepdims=True)
    variance = jnp.mean((values - mean_value) ** 2, axis=-1, keepdims=True)
    return ((values - mean_value) * lax.rsqrt(variance + 1e-05) * norm_gain + norm_bias).astype(
        jnp.bfloat16
    )


def grid_bias(position_bias, grid_side):
    position = jnp.arange(grid_side * grid_side, dtype=jnp.int32)
    row_of = position // grid_side
    col_of = position % grid_side
    offset_index = (row_of[:, None] - row_of[None, :] + grid_side - 1) * (2 * grid_side - 1) + (
        col_of[:, None] - col_of[None, :] + grid_side - 1
    )
    return jnp.take(position_bias, offset_index, axis=1)


def attend(projected, table, head_count):
    group_count, tokens, triple = projected.shape
    channels = triple // 3
    head_size = channels // head_count
    split_parts = projected.reshape(group_count, tokens, 3, head_count, head_size)
    query_part = split_parts[:, :, 0]
    key_part = split_parts[:, :, 1]
    value_part = split_parts[:, :, 2]
    scores = (
        jnp.einsum("nqhd,nkhd->nhqk", query_part, key_part, preferred_element_type=jnp.float32)
        * head_size ** (-0.5)
        + table[None]
    )
    probs = jax.nn.softmax(scores, axis=-1).astype(jnp.bfloat16)
    attended = jnp.einsum("nhqk,nkhd->nqhd", probs, value_part, preferred_element_type=jnp.float32)
    return attended.astype(jnp.bfloat16).reshape(group_count, tokens, channels)


def attention_kernel(x_ref, w_ref, bias_ref, o_ref):
    block, tokens, channels = x_ref.shape
    head_size = channels // HEADS
    x = x_ref[...].reshape(block * tokens, channels)
    qkv = jnp.dot(x, w_ref[...], preferred_element_type=jnp.float32).astype(jnp.bfloat16)
    query = qkv[:, :channels]
    key = qkv[:, channels : 2 * channels].reshape(block, tokens, channels)
    value = qkv[:, 2 * channels :]
    head_of = lax.broadcasted_iota(jnp.int32, (1, channels), 1) // head_size
    out = jnp.zeros((block, tokens, channels), jnp.float32)
    for head in range(HEADS):
        mask = head_of == head
        masked_query = jnp.where(mask, query, jnp.zeros_like(query)).reshape(block, tokens, channels)
        scores = (
            jnp.einsum("gtd,gud->gtu", masked_query, key, preferred_element_type=jnp.float32)
            * head_size ** (-0.5)
            + bias_ref[head][None]
        )
        shifted = jnp.exp(scores - jnp.max(scores, axis=-1, keepdims=True))
        probs = (shifted / jnp.sum(shifted, axis=-1, keepdims=True)).astype(jnp.bfloat16)
        masked_value = jnp.where(mask, value, jnp.zeros_like(value)).reshape(block, tokens, channels)
        part = jnp.einsum("gtu,gud->gtd", probs, masked_value, preferred_element_type=jnp.float32)
        out = jnp.where(mask.reshape(1, 1, channels), part, out)
    o_ref[...] = out.astype(o_ref.dtype)


def grid_attention(grouped, mixing_weight, table):
    count, tokens, channels = grouped.shape
    block = next(b for b in (32, 16, 8, 4, 2, 1) if count % b == 0)
    return pl.pallas_call(
        attention_kernel,
        grid=(count // block,),
        in_specs=[
            pl.BlockSpec((block, tokens, channels), lambda i: (i, 0, 0)),
            pl.BlockSpec(mixing_weight.shape, lambda i: (0, 0)),
            pl.BlockSpec(table.shape, lambda i: (0, 0, 0)),
        ],
        out_specs=pl.BlockSpec((block, tokens, channels), lambda i: (i, 0, 0)),
        out_shape=jax.ShapeDtypeStruct((count, tokens, channels), jnp.bfloat16),
    )(grouped, mixing_weight, table)


def pieces_of(normed, row_size, col_size, pp, span, col_count, channels):
    across = G // col_size
    inner_cols = col_count // across // col_size
    return (
        normed.reshape(row_size, pp, across, col_size, inner_cols, channels)
        .transpose(0, 3, 1, 2, 4, 5)
        .reshape(row_size * col_size, pp, across, inner_cols, channels)
    )


def body(
    sky_map,
    expand_weight,
    expand_bias,
    depth_weight,
    depth_bias,
    project_weight,
    project_bias,
    norm_gain,
    norm_bias,
    mixing_weight,
    position_bias,
    output_weight,
):
    row_count, col_count, channels = sky_map.shape
    row_size = lax.axis_size("row")
    expanded = expand_layer(sky_map, expand_weight, expand_bias)
    padded = with_halo(expanded, (("row", 0), ("col", 1)), 1)
    across = G // lax.axis_size("col")
    stride = col_count // across
    table = grid_bias(position_bias, G)
    pieces = next(n for n in (4, 2, 1) if row_count % (n * row_size) == 0 and (row_count // n) % G == 0)
    span = row_count // pieces
    col_size = lax.axis_size("col")
    sub = row_size // G
    pp = span // row_size
    inner_cols = stride // col_size
    windows = [padded[piece * span : piece * span + span + 2] for piece in range(pieces)]
    outs = []
    for piece in range(pieces):
        first = piece * span
        hidden = depthwise(windows[piece], depth_weight, depth_bias, span, col_count)
        after_conv = (
            sky_map[first : first + span].astype(jnp.float32)
            + jnp.dot(hidden, project_weight, preferred_element_type=jnp.float32)
            + project_bias
        ).astype(jnp.bfloat16)
        normed = layer_norm(after_conv, norm_gain, norm_bias)
        pair = pieces_of(normed, row_size, col_size, pp, span, col_count, channels)
        if piece + 1 < pieces:
            pair, windows[piece + 1] = lax.optimization_barrier((pair, windows[piece + 1]))
        moved = lax.all_to_all(pair, ("row", "col"), 0, 0, tiled=True)
        grouped = (
            moved.reshape(G, sub, col_size, pp, across, inner_cols, channels)
            .transpose(1, 3, 5, 0, 2, 4, 6)
            .reshape(sub * pp * inner_cols, G * G, channels)
        )
        heads_out = grid_attention(grouped, mixing_weight, table)
        returned = (
            heads_out.reshape(sub, pp, inner_cols, G, col_size, across, channels)
            .transpose(3, 0, 4, 1, 5, 2, 6)
            .reshape(row_size * col_size, pp, across, inner_cols, channels)
        )
        returned = lax.all_to_all(returned, ("row", "col"), 0, 0, tiled=True)
        returned = (
            returned.reshape(row_size, col_size, pp, across, inner_cols, channels)
            .transpose(0, 2, 3, 1, 4, 5)
            .reshape(span, col_count, channels)
        )
        outs.append(
            (
                after_conv.astype(jnp.float32)
                + jnp.dot(returned, output_weight, preferred_element_type=jnp.float32)
            ).astype(jnp.bfloat16)
        )
    return jnp.concatenate(outs, axis=0)


def solution(mesh):
    placed = (
        P(("groups", "row"), "col", None),
        P(),
        P(),
        P(),
        P(),
        P(),
        P(),
        P(),
        P(),
        P(),
        P(),
        P(),
    )
    return jax.shard_map(
        body,
        mesh=mesh,
        in_specs=placed,
        out_specs=P(("groups", "row"), "col", None),
        check_vma=False,
    )
```

```python
import jax
import jax.numpy as jnp
from jax import lax
from jax.sharding import PartitionSpec as P
from jax.experimental import pallas as pl

HEADS = 4
G = 8


def with_halo(array, sides, width):
    for axis, dim in sides:
        size, length = (lax.axis_size(axis), array.shape[dim])
        up = [(i, (i + 1) % size) for i in range(size - 1)]
        down = [(j, i) for i, j in up]
        last = lax.slice_in_dim(array, length - width, length, axis=dim)
        initial = lax.slice_in_dim(array, 0, width, axis=dim)
        before = lax.ppermute(last, axis, up)
        after = lax.ppermute(initial, axis, down)
        array = jnp.concatenate([before, array, after], axis=dim)
    return array


def gelu_tanh(values):
    return jax.nn.gelu(values, approximate=True)


def expand_layer(features, expand_weight, expand_bias):
    return gelu_tanh(
        jnp.dot(features, expand_weight, preferred_element_type=jnp.float32) + expand_bias
    ).astype(jnp.bfloat16)


def depthwise(padded, depth_weight, depth_bias, row_count, col_count):
    accumulated = jnp.zeros((row_count, col_count, padded.shape[2]), jnp.float32) + depth_bias
    for row_shift in range(3):
        for col_shift in range(3):
            accumulated = (
                accumulated
                + padded[row_shift : row_shift + row_count, col_shift : col_shift + col_count]
                * depth_weight[row_shift, col_shift]
            )
    return gelu_tanh(accumulated).astype(jnp.bfloat16)


def layer_norm(features, norm_gain, norm_bias):
    values = features.astype(jnp.float32)
    mean_value = jnp.mean(values, axis=-1, keepdims=True)
    variance = jnp.mean((values - mean_value) ** 2, axis=-1, keepdims=True)
    return ((values - mean_value) * lax.rsqrt(variance + 1e-05) * norm_gain + norm_bias).astype(
        jnp.bfloat16
    )


def grid_bias(position_bias, grid_side):
    position = jnp.arange(grid_side * grid_side, dtype=jnp.int32)
    row_of = position // grid_side
    col_of = position % grid_side
    offset_index = (row_of[:, None] - row_of[None, :] + grid_side - 1) * (2 * grid_side - 1) + (
        col_of[:, None] - col_of[None, :] + grid_side - 1
    )
    return jnp.take(position_bias, offset_index, axis=1)


def attend(projected, table, head_count):
    group_count, tokens, triple = projected.shape
    channels = triple // 3
    head_size = channels // head_count
    split_parts = projected.reshape(group_count, tokens, 3, head_count, head_size)
    query_part = split_parts[:, :, 0]
    key_part = split_parts[:, :, 1]
    value_part = split_parts[:, :, 2]
    scores = (
        jnp.einsum("nqhd,nkhd->nhqk", query_part, key_part, preferred_element_type=jnp.float32)
        * head_size ** (-0.5)
        + table[None]
    )
    probs = jax.nn.softmax(scores, axis=-1).astype(jnp.bfloat16)
    attended = jnp.einsum("nhqk,nkhd->nqhd", probs, value_part, preferred_element_type=jnp.float32)
    return attended.astype(jnp.bfloat16).reshape(group_count, tokens, channels)


def attention_kernel(x_ref, w_ref, bias_ref, o_ref):
    block, tokens, channels = x_ref.shape
    head_size = channels // HEADS
    x = x_ref[...].reshape(block * tokens, channels)
    qkv = jnp.dot(x, w_ref[...], preferred_element_type=jnp.float32).astype(jnp.bfloat16)
    query = qkv[:, :channels]
    key = qkv[:, channels : 2 * channels].reshape(block, tokens, channels)
    value = qkv[:, 2 * channels :]
    head_of = lax.broadcasted_iota(jnp.int32, (1, channels), 1) // head_size
    out = jnp.zeros((block, tokens, channels), jnp.float32)
    for head in range(HEADS):
        mask = head_of == head
        masked_query = jnp.where(mask, query, jnp.zeros_like(query)).reshape(block, tokens, channels)
        scores = (
            jnp.einsum("gtd,gud->gtu", masked_query, key, preferred_element_type=jnp.float32)
            * head_size ** (-0.5)
            + bias_ref[head][None]
        )
        shifted = jnp.exp(scores - jnp.max(scores, axis=-1, keepdims=True))
        probs = (shifted / jnp.sum(shifted, axis=-1, keepdims=True)).astype(jnp.bfloat16)
        masked_value = jnp.where(mask, value, jnp.zeros_like(value)).reshape(block, tokens, channels)
        part = jnp.einsum("gtu,gud->gtd", probs, masked_value, preferred_element_type=jnp.float32)
        out = jnp.where(mask.reshape(1, 1, channels), part, out)
    o_ref[...] = out.astype(o_ref.dtype)


def grid_attention(grouped, mixing_weight, table):
    count, tokens, channels = grouped.shape
    block = next(b for b in (32, 16, 8, 4, 2, 1) if count % b == 0)
    return pl.pallas_call(
        attention_kernel,
        grid=(count // block,),
        in_specs=[
            pl.BlockSpec((block, tokens, channels), lambda i: (i, 0, 0)),
            pl.BlockSpec(mixing_weight.shape, lambda i: (0, 0)),
            pl.BlockSpec(table.shape, lambda i: (0, 0, 0)),
        ],
        out_specs=pl.BlockSpec((block, tokens, channels), lambda i: (i, 0, 0)),
        out_shape=jax.ShapeDtypeStruct((count, tokens, channels), jnp.bfloat16),
    )(grouped, mixing_weight, table)


def pieces_of(normed, row_size, col_size, pp, span, col_count, channels):
    across = G // col_size
    inner_cols = col_count // across // col_size
    return (
        normed.reshape(row_size, pp, across, col_size, inner_cols, channels)
        .transpose(0, 3, 1, 2, 4, 5)
        .reshape(row_size * col_size, pp, across, inner_cols, channels)
    )


def expanded_window(expanded, edges, first, span):
    top, bottom, left, right = edges
    rows = jnp.concatenate([top, expanded, bottom], axis=0)[first : first + span + 2]
    return jnp.concatenate(
        [left[first : first + span + 2], rows, right[first : first + span + 2]], axis=1
    )


def expanded_edges(sky_map, expand_weight, expand_bias):
    row_size, col_size = lax.axis_size("row"), lax.axis_size("col")
    row_at, col_at = lax.axis_index("row"), lax.axis_index("col")
    row_count = sky_map.shape[0]
    up = [(i, i + 1) for i in range(row_size - 1)]
    top = lax.ppermute(sky_map[row_count - 1 :], "row", up)
    bottom = lax.ppermute(sky_map[:1], "row", [(j, i) for i, j in up])
    rows = jnp.concatenate([top, sky_map, bottom], axis=0)
    right_of = [(i, i + 1) for i in range(col_size - 1)]
    left = lax.ppermute(rows[:, -1:], "col", right_of)
    right = lax.ppermute(rows[:, :1], "col", [(j, i) for i, j in right_of])
    row_ok = jnp.concatenate(
        [
            jnp.full((1,), row_at > 0),
            jnp.full((row_count,), True),
            jnp.full((1,), row_at < row_size - 1),
        ]
    )[:, None, None]

    def grown(cells, valid):
        return jnp.where(valid, expand_layer(cells, expand_weight, expand_bias), jnp.zeros((), jnp.bfloat16))

    return (
        grown(top, row_at > 0),
        grown(bottom, row_at < row_size - 1),
        grown(left, row_ok & (col_at > 0)),
        grown(right, row_ok & (col_at < col_size - 1)),
    )


def body(
    sky_map,
    expand_weight,
    expand_bias,
    depth_weight,
    depth_bias,
    project_weight,
    project_bias,
    norm_gain,
    norm_bias,
    mixing_weight,
    position_bias,
    output_weight,
):
    row_count, col_count, channels = sky_map.shape
    row_size = lax.axis_size("row")
    expanded = expand_layer(sky_map, expand_weight, expand_bias)
    edges = expanded_edges(sky_map, expand_weight, expand_bias)
    across = G // lax.axis_size("col")
    stride = col_count // across
    table = grid_bias(position_bias, G)
    pieces = 2 if row_count % (2 * row_size) == 0 and (row_count // 2) % G == 0 else 1
    span = row_count // pieces
    col_size = lax.axis_size("col")
    sub = row_size // G
    pp = span // row_size
    inner_cols = stride // col_size
    source = expanded
    outs = []
    for piece in range(pieces):
        first = piece * span
        window = expanded_window(source, edges, first, span)
        hidden = depthwise(window, depth_weight, depth_bias, span, col_count)
        after_conv = (
            sky_map[first : first + span].astype(jnp.float32)
            + jnp.dot(hidden, project_weight, preferred_element_type=jnp.float32)
            + project_bias
        ).astype(jnp.bfloat16)
        normed = layer_norm(after_conv, norm_gain, norm_bias)
        pair = pieces_of(normed, row_size, col_size, pp, span, col_count, channels)
        if piece + 1 < pieces:
            pair, source = lax.optimization_barrier((pair, expanded))
        moved = lax.all_to_all(pair, ("row", "col"), 0, 0, tiled=True)
        grouped = (
            moved.reshape(G, sub, col_size, pp, across, inner_cols, channels)
            .transpose(1, 3, 5, 0, 2, 4, 6)
            .reshape(sub * pp * inner_cols, G * G, channels)
        )
        heads_out = grid_attention(grouped, mixing_weight, table)
        returned = (
            heads_out.reshape(sub, pp, inner_cols, G, col_size, across, channels)
            .transpose(3, 0, 4, 1, 5, 2, 6)
            .reshape(row_size * col_size, pp, across, inner_cols, channels)
        )
        returned = lax.all_to_all(returned, ("row", "col"), 0, 0, tiled=True)
        returned = (
            returned.reshape(row_size, col_size, pp, across, inner_cols, channels)
            .transpose(0, 2, 3, 1, 4, 5)
            .reshape(span, col_count, channels)
        )
        outs.append(
            (
                after_conv.astype(jnp.float32)
                + jnp.dot(returned, output_weight, preferred_element_type=jnp.float32)
            ).astype(jnp.bfloat16)
        )
    return jnp.concatenate(outs, axis=0)


def solution(mesh):
    placed = (
        P(("groups", "row"), "col", None),
        P(),
        P(),
        P(),
        P(),
        P(),
        P(),
        P(),
        P(),
        P(),
        P(),
        P(),
    )
    return jax.shard_map(
        body,
        mesh=mesh,
        in_specs=placed,
        out_specs=P(("groups", "row"), "col", None),
        check_vma=False,
    )
```

```python
import jax
import jax.numpy as jnp
from jax import lax
from jax.sharding import PartitionSpec as P
from jax.experimental import pallas as pl

HEADS = 4
G = 8


def with_halo(array, sides, width):
    for axis, dim in sides:
        size, length = (lax.axis_size(axis), array.shape[dim])
        up = [(i, (i + 1) % size) for i in range(size - 1)]
        down = [(j, i) for i, j in up]
        last = lax.slice_in_dim(array, length - width, length, axis=dim)
        initial = lax.slice_in_dim(array, 0, width, axis=dim)
        before = lax.ppermute(last, axis, up)
        after = lax.ppermute(initial, axis, down)
        array = jnp.concatenate([before, array, after], axis=dim)
    return array


def gelu_tanh(values):
    return jax.nn.gelu(values, approximate=True)


def expand_layer(features, expand_weight, expand_bias):
    return gelu_tanh(
        jnp.dot(features, expand_weight, preferred_element_type=jnp.float32) + expand_bias
    ).astype(jnp.bfloat16)


def depthwise(padded, depth_weight, depth_bias, row_count, col_count):
    accumulated = jnp.zeros((row_count, col_count, padded.shape[2]), jnp.float32) + depth_bias
    for row_shift in range(3):
        for col_shift in range(3):
            accumulated = (
                accumulated
                + padded[row_shift : row_shift + row_count, col_shift : col_shift + col_count]
                * depth_weight[row_shift, col_shift]
            )
    return gelu_tanh(accumulated).astype(jnp.bfloat16)


def layer_norm(features, norm_gain, norm_bias):
    values = features.astype(jnp.float32)
    mean_value = jnp.mean(values, axis=-1, keepdims=True)
    variance = jnp.mean((values - mean_value) ** 2, axis=-1, keepdims=True)
    return ((values - mean_value) * lax.rsqrt(variance + 1e-05) * norm_gain + norm_bias).astype(
        jnp.bfloat16
    )


def grid_bias(position_bias, grid_side):
    position = jnp.arange(grid_side * grid_side, dtype=jnp.int32)
    row_of = position // grid_side
    col_of = position % grid_side
    offset_index = (row_of[:, None] - row_of[None, :] + grid_side - 1) * (2 * grid_side - 1) + (
        col_of[:, None] - col_of[None, :] + grid_side - 1
    )
    return jnp.take(position_bias, offset_index, axis=1)


def attend(projected, table, head_count):
    group_count, tokens, triple = projected.shape
    channels = triple // 3
    head_size = channels // head_count
    split_parts = projected.reshape(group_count, tokens, 3, head_count, head_size)
    query_part = split_parts[:, :, 0]
    key_part = split_parts[:, :, 1]
    value_part = split_parts[:, :, 2]
    scores = (
        jnp.einsum("nqhd,nkhd->nhqk", query_part, key_part, preferred_element_type=jnp.float32)
        * head_size ** (-0.5)
        + table[None]
    )
    probs = jax.nn.softmax(scores, axis=-1).astype(jnp.bfloat16)
    attended = jnp.einsum("nhqk,nkhd->nqhd", probs, value_part, preferred_element_type=jnp.float32)
    return attended.astype(jnp.bfloat16).reshape(group_count, tokens, channels)


def attention_kernel(x_ref, w_ref, bias_ref, o_ref):
    block, tokens, channels = x_ref.shape
    head_size = channels // HEADS
    x = x_ref[...].reshape(block * tokens, channels)
    qkv = jnp.dot(x, w_ref[...], preferred_element_type=jnp.float32).astype(jnp.bfloat16)
    query = qkv[:, :channels]
    key = qkv[:, channels : 2 * channels].reshape(block, tokens, channels)
    value = qkv[:, 2 * channels :]
    head_of = lax.broadcasted_iota(jnp.int32, (1, channels), 1) // head_size
    out = jnp.zeros((block, tokens, channels), jnp.float32)
    for head in range(HEADS):
        mask = head_of == head
        masked_query = jnp.where(mask, query, jnp.zeros_like(query)).reshape(block, tokens, channels)
        scores = (
            jnp.einsum("gtd,gud->gtu", masked_query, key, preferred_element_type=jnp.float32)
            * head_size ** (-0.5)
            + bias_ref[head][None]
        )
        shifted = jnp.exp(scores - jnp.max(scores, axis=-1, keepdims=True))
        probs = (shifted / jnp.sum(shifted, axis=-1, keepdims=True)).astype(jnp.bfloat16)
        masked_value = jnp.where(mask, value, jnp.zeros_like(value)).reshape(block, tokens, channels)
        part = jnp.einsum("gtu,gud->gtd", probs, masked_value, preferred_element_type=jnp.float32)
        out = jnp.where(mask.reshape(1, 1, channels), part, out)
    o_ref[...] = out.astype(o_ref.dtype)


def grid_attention(grouped, mixing_weight, table):
    count, tokens, channels = grouped.shape
    block = next(b for b in (32, 16, 8, 4, 2, 1) if count % b == 0)
    return pl.pallas_call(
        attention_kernel,
        grid=(count // block,),
        in_specs=[
            pl.BlockSpec((block, tokens, channels), lambda i: (i, 0, 0)),
            pl.BlockSpec(mixing_weight.shape, lambda i: (0, 0)),
            pl.BlockSpec(table.shape, lambda i: (0, 0, 0)),
        ],
        out_specs=pl.BlockSpec((block, tokens, channels), lambda i: (i, 0, 0)),
        out_shape=jax.ShapeDtypeStruct((count, tokens, channels), jnp.bfloat16),
    )(grouped, mixing_weight, table)


def pieces_of(normed, row_size, col_size, pp, span, col_count, channels):
    across = G // col_size
    inner_cols = col_count // across // col_size
    return (
        normed.reshape(row_size, pp, across, col_size, inner_cols, channels)
        .transpose(0, 3, 1, 2, 4, 5)
        .reshape(row_size * col_size, pp, across, inner_cols, channels)
    )


def expanded_window(expanded, edges, first, span):
    top, bottom, left, right = edges
    rows = jnp.concatenate([top, expanded, bottom], axis=0)[first : first + span + 2]
    return jnp.concatenate(
        [left[first : first + span + 2], rows, right[first : first + span + 2]], axis=1
    )


def expanded_edges(sky_map, expand_weight, expand_bias):
    row_size, col_size = lax.axis_size("row"), lax.axis_size("col")
    row_at, col_at = lax.axis_index("row"), lax.axis_index("col")
    row_count = sky_map.shape[0]
    up = [(i, i + 1) for i in range(row_size - 1)]
    top = lax.ppermute(sky_map[row_count - 1], "row", up)[None]
    bottom = lax.ppermute(sky_map[0], "row", [(j, i) for i, j in up])[None]
    last_col = jnp.concatenate([top[:, -1], sky_map[:, -1], bottom[:, -1]], axis=0)
    first_col = jnp.concatenate([top[:, 0], sky_map[:, 0], bottom[:, 0]], axis=0)
    right_of = [(i, i + 1) for i in range(col_size - 1)]
    left = lax.ppermute(last_col, "col", right_of)[:, None]
    right = lax.ppermute(first_col, "col", [(j, i) for i, j in right_of])[:, None]
    row_ok = jnp.concatenate(
        [
            jnp.full((1,), row_at > 0),
            jnp.full((row_count,), True),
            jnp.full((1,), row_at < row_size - 1),
        ]
    )[:, None, None]

    def grown(cells, valid):
        return jnp.where(valid, expand_layer(cells, expand_weight, expand_bias), jnp.zeros((), jnp.bfloat16))

    return (
        grown(top, row_at > 0),
        grown(bottom, row_at < row_size - 1),
        grown(left, row_ok & (col_at > 0)),
        grown(right, row_ok & (col_at < col_size - 1)),
    )


def body(
    sky_map,
    expand_weight,
    expand_bias,
    depth_weight,
    depth_bias,
    project_weight,
    project_bias,
    norm_gain,
    norm_bias,
    mixing_weight,
    position_bias,
    output_weight,
):
    row_count, col_count, channels = sky_map.shape
    row_size = lax.axis_size("row")
    expanded = expand_layer(sky_map, expand_weight, expand_bias)
    edges = expanded_edges(sky_map, expand_weight, expand_bias)
    across = G // lax.axis_size("col")
    stride = col_count // across
    table = grid_bias(position_bias, G)
    pieces = 2 if row_count % (2 * row_size) == 0 and (row_count // 2) % G == 0 else 1
    span = row_count // pieces
    col_size = lax.axis_size("col")
    sub = row_size // G
    pp = span // row_size
    inner_cols = stride // col_size
    source = expanded
    outs = []
    for piece in range(pieces):
        first = piece * span
        window = expanded_window(source, edges, first, span)
        hidden = depthwise(window, depth_weight, depth_bias, span, col_count)
        after_conv = (
            sky_map[first : first + span].astype(jnp.float32)
            + jnp.dot(hidden, project_weight, preferred_element_type=jnp.float32)
            + project_bias
        ).astype(jnp.bfloat16)
        normed = layer_norm(after_conv, norm_gain, norm_bias)
        pair = pieces_of(normed, row_size, col_size, pp, span, col_count, channels)
        if piece + 1 < pieces:
            pair, source = lax.optimization_barrier((pair, expanded))
        moved = lax.all_to_all(pair, ("row", "col"), 0, 0, tiled=True)
        grouped = (
            moved.reshape(G, sub, col_size, pp, across, inner_cols, channels)
            .transpose(1, 3, 5, 0, 2, 4, 6)
            .reshape(sub * pp * inner_cols, G * G, channels)
        )
        heads_out = grid_attention(grouped, mixing_weight, table)
        returned = (
            heads_out.reshape(sub, pp, inner_cols, G, col_size, across, channels)
            .transpose(3, 0, 4, 1, 5, 2, 6)
            .reshape(row_size * col_size, pp, across, inner_cols, channels)
        )
        returned = lax.all_to_all(returned, ("row", "col"), 0, 0, tiled=True)
        returned = (
            returned.reshape(row_size, col_size, pp, across, inner_cols, channels)
            .transpose(0, 2, 3, 1, 4, 5)
            .reshape(span, col_count, channels)
        )
        outs.append(
            (
                after_conv.astype(jnp.float32)
                + jnp.dot(returned, output_weight, preferred_element_type=jnp.float32)
            ).astype(jnp.bfloat16)
        )
    return jnp.concatenate(outs, axis=0)


def solution(mesh):
    placed = (
        P(("groups", "row"), "col", None),
        P(),
        P(),
        P(),
        P(),
        P(),
        P(),
        P(),
        P(),
        P(),
        P(),
        P(),
    )
    return jax.shard_map(
        body,
        mesh=mesh,
        in_specs=placed,
        out_specs=P(("groups", "row"), "col", None),
        check_vma=False,
    )
```

```python
import jax
import jax.numpy as jnp
from jax import lax
from jax.sharding import PartitionSpec as P
from jax.experimental import pallas as pl

HEADS = 4
G = 8


def with_halo(array, sides, width):
    for axis, dim in sides:
        size, length = (lax.axis_size(axis), array.shape[dim])
        up = [(i, (i + 1) % size) for i in range(size - 1)]
        down = [(j, i) for i, j in up]
        last = lax.slice_in_dim(array, length - width, length, axis=dim)
        initial = lax.slice_in_dim(array, 0, width, axis=dim)
        before = lax.ppermute(last, axis, up)
        after = lax.ppermute(initial, axis, down)
        array = jnp.concatenate([before, array, after], axis=dim)
    return array


def gelu_tanh(values):
    return jax.nn.gelu(values, approximate=True)


def expand_layer(features, expand_weight, expand_bias):
    return gelu_tanh(
        jnp.dot(features, expand_weight, preferred_element_type=jnp.float32) + expand_bias
    ).astype(jnp.bfloat16)


def depthwise(padded, depth_weight, depth_bias, row_count, col_count):
    accumulated = jnp.zeros((row_count, col_count, padded.shape[2]), jnp.float32) + depth_bias
    for row_shift in range(3):
        for col_shift in range(3):
            accumulated = (
                accumulated
                + padded[row_shift : row_shift + row_count, col_shift : col_shift + col_count]
                * depth_weight[row_shift, col_shift]
            )
    return gelu_tanh(accumulated).astype(jnp.bfloat16)


def layer_norm(features, norm_gain, norm_bias):
    values = features.astype(jnp.float32)
    mean_value = jnp.mean(values, axis=-1, keepdims=True)
    variance = jnp.mean((values - mean_value) ** 2, axis=-1, keepdims=True)
    return ((values - mean_value) * lax.rsqrt(variance + 1e-05) * norm_gain + norm_bias).astype(
        jnp.bfloat16
    )


def grid_bias(position_bias, grid_side):
    position = jnp.arange(grid_side * grid_side, dtype=jnp.int32)
    row_of = position // grid_side
    col_of = position % grid_side
    offset_index = (row_of[:, None] - row_of[None, :] + grid_side - 1) * (2 * grid_side - 1) + (
        col_of[:, None] - col_of[None, :] + grid_side - 1
    )
    return jnp.take(position_bias, offset_index, axis=1)


def attend(projected, table, head_count):
    group_count, tokens, triple = projected.shape
    channels = triple // 3
    head_size = channels // head_count
    split_parts = projected.reshape(group_count, tokens, 3, head_count, head_size)
    query_part = split_parts[:, :, 0]
    key_part = split_parts[:, :, 1]
    value_part = split_parts[:, :, 2]
    scores = (
        jnp.einsum("nqhd,nkhd->nhqk", query_part, key_part, preferred_element_type=jnp.float32)
        * head_size ** (-0.5)
        + table[None]
    )
    probs = jax.nn.softmax(scores, axis=-1).astype(jnp.bfloat16)
    attended = jnp.einsum("nhqk,nkhd->nqhd", probs, value_part, preferred_element_type=jnp.float32)
    return attended.astype(jnp.bfloat16).reshape(group_count, tokens, channels)


def attention_kernel(x_ref, w_ref, bias_ref, o_ref):
    block, tokens, channels = x_ref.shape
    head_size = channels // HEADS
    x = x_ref[...].reshape(block * tokens, channels)
    qkv = jnp.dot(x, w_ref[...], preferred_element_type=jnp.float32).astype(jnp.bfloat16)
    query = qkv[:, :channels]
    key = qkv[:, channels : 2 * channels].reshape(block, tokens, channels)
    value = qkv[:, 2 * channels :]
    head_of = lax.broadcasted_iota(jnp.int32, (1, channels), 1) // head_size
    out = jnp.zeros((block, tokens, channels), jnp.float32)
    for head in range(HEADS):
        mask = head_of == head
        masked_query = jnp.where(mask, query, jnp.zeros_like(query)).reshape(block, tokens, channels)
        scores = (
            jnp.einsum("gtd,gud->gtu", masked_query, key, preferred_element_type=jnp.float32)
            * head_size ** (-0.5)
            + bias_ref[head][None]
        )
        shifted = jnp.exp(scores - jnp.max(scores, axis=-1, keepdims=True))
        probs = (shifted / jnp.sum(shifted, axis=-1, keepdims=True)).astype(jnp.bfloat16)
        masked_value = jnp.where(mask, value, jnp.zeros_like(value)).reshape(block, tokens, channels)
        part = jnp.einsum("gtu,gud->gtd", probs, masked_value, preferred_element_type=jnp.float32)
        out = jnp.where(mask.reshape(1, 1, channels), part, out)
    o_ref[...] = out.astype(o_ref.dtype)


def grid_attention(grouped, mixing_weight, table):
    count, tokens, channels = grouped.shape
    block = next(b for b in (32, 16, 8, 4, 2, 1) if count % b == 0)
    return pl.pallas_call(
        attention_kernel,
        grid=(count // block,),
        in_specs=[
            pl.BlockSpec((block, tokens, channels), lambda i: (i, 0, 0)),
            pl.BlockSpec(mixing_weight.shape, lambda i: (0, 0)),
            pl.BlockSpec(table.shape, lambda i: (0, 0, 0)),
        ],
        out_specs=pl.BlockSpec((block, tokens, channels), lambda i: (i, 0, 0)),
        out_shape=jax.ShapeDtypeStruct((count, tokens, channels), jnp.bfloat16),
    )(grouped, mixing_weight, table)


def pieces_of(normed, row_size, col_size, pp, span, col_count, channels):
    across = G // col_size
    inner_cols = col_count // across // col_size
    return (
        normed.reshape(row_size, pp, across, col_size, inner_cols, channels)
        .transpose(0, 3, 1, 2, 4, 5)
        .reshape(row_size * col_size, pp, across, inner_cols, channels)
    )


def expanded_window(expanded, edges, first, span):
    top, bottom, left, right = edges
    rows = jnp.concatenate([top, expanded, bottom], axis=0)[first : first + span + 2]
    return jnp.concatenate(
        [left[first : first + span + 2], rows, right[first : first + span + 2]], axis=1
    )


def expanded_edges(sky_map, expand_weight, expand_bias):
    row_size, col_size = lax.axis_size("row"), lax.axis_size("col")
    row_at, col_at = lax.axis_index("row"), lax.axis_index("col")
    row_count = sky_map.shape[0]
    up = [(i, i + 1) for i in range(row_size - 1)]
    top = lax.ppermute(sky_map[row_count - 1], "row", up)[None]
    bottom = lax.ppermute(sky_map[0], "row", [(j, i) for i, j in up])[None]
    last_col = jnp.concatenate([top[:, -1], sky_map[:, -1], bottom[:, -1]], axis=0)
    first_col = jnp.concatenate([top[:, 0], sky_map[:, 0], bottom[:, 0]], axis=0)
    right_of = [(i, i + 1) for i in range(col_size - 1)]
    left = lax.ppermute(last_col, "col", right_of)[:, None]
    right = lax.ppermute(first_col, "col", [(j, i) for i, j in right_of])[:, None]
    row_ok = jnp.concatenate(
        [
            jnp.full((1,), row_at > 0),
            jnp.full((row_count,), True),
            jnp.full((1,), row_at < row_size - 1),
        ]
    )[:, None, None]

    def grown(cells, valid):
        return jnp.where(valid, expand_layer(cells, expand_weight, expand_bias), jnp.zeros((), jnp.bfloat16))

    return (
        grown(top, row_at > 0),
        grown(bottom, row_at < row_size - 1),
        grown(left, row_ok & (col_at > 0)),
        grown(right, row_ok & (col_at < col_size - 1)),
    )


def body(
    sky_map,
    expand_weight,
    expand_bias,
    depth_weight,
    depth_bias,
    project_weight,
    project_bias,
    norm_gain,
    norm_bias,
    mixing_weight,
    position_bias,
    output_weight,
):
    row_count, col_count, channels = sky_map.shape
    row_size = lax.axis_size("row")
    expanded = expand_layer(sky_map, expand_weight, expand_bias)
    edges = expanded_edges(sky_map, expand_weight, expand_bias)
    across = G // lax.axis_size("col")
    stride = col_count // across
    table = grid_bias(position_bias, G)
    if row_count % row_size == 0 and row_count > row_size:
        spans = [row_size, row_count - row_size]
    else:
        spans = [row_count]
    pieces = len(spans)
    col_size = lax.axis_size("col")
    sub = row_size // G
    inner_cols = stride // col_size
    source = expanded
    outs = []
    for piece in range(pieces):
        first = sum(spans[:piece])
        span = spans[piece]
        pp = span // row_size
        window = expanded_window(source, edges, first, span)
        hidden = depthwise(window, depth_weight, depth_bias, span, col_count)
        after_conv = (
            sky_map[first : first + span].astype(jnp.float32)
            + jnp.dot(hidden, project_weight, preferred_element_type=jnp.float32)
            + project_bias
        ).astype(jnp.bfloat16)
        normed = layer_norm(after_conv, norm_gain, norm_bias)
        pair = pieces_of(normed, row_size, col_size, pp, span, col_count, channels)
        if piece + 1 < pieces:
            pair, source = lax.optimization_barrier((pair, expanded))
        moved = lax.all_to_all(pair, ("row", "col"), 0, 0, tiled=True)
        grouped = (
            moved.reshape(G, sub, col_size, pp, across, inner_cols, channels)
            .transpose(1, 3, 5, 0, 2, 4, 6)
            .reshape(sub * pp * inner_cols, G * G, channels)
        )
        heads_out = grid_attention(grouped, mixing_weight, table)
        returned = (
            heads_out.reshape(sub, pp, inner_cols, G, col_size, across, channels)
            .transpose(3, 0, 4, 1, 5, 2, 6)
            .reshape(row_size * col_size, pp, across, inner_cols, channels)
        )
        returned = lax.all_to_all(returned, ("row", "col"), 0, 0, tiled=True)
        returned = (
            returned.reshape(row_size, col_size, pp, across, inner_cols, channels)
            .transpose(0, 2, 3, 1, 4, 5)
            .reshape(span, col_count, channels)
        )
        outs.append(
            (
                after_conv.astype(jnp.float32)
                + jnp.dot(returned, output_weight, preferred_element_type=jnp.float32)
            ).astype(jnp.bfloat16)
        )
    return jnp.concatenate(outs, axis=0)


def solution(mesh):
    placed = (
        P(("groups", "row"), "col", None),
        P(),
        P(),
        P(),
        P(),
        P(),
        P(),
        P(),
        P(),
        P(),
        P(),
        P(),
    )
    return jax.shard_map(
        body,
        mesh=mesh,
        in_specs=placed,
        out_specs=P(("groups", "row"), "col", None),
        check_vma=False,
    )
```

```python
import jax
import jax.numpy as jnp
from jax import lax
from jax.sharding import PartitionSpec as P
from jax.experimental import pallas as pl

HEADS = 4
G = 8


def with_halo(array, sides, width):
    for axis, dim in sides:
        size, length = (lax.axis_size(axis), array.shape[dim])
        up = [(i, (i + 1) % size) for i in range(size - 1)]
        down = [(j, i) for i, j in up]
        last = lax.slice_in_dim(array, length - width, length, axis=dim)
        initial = lax.slice_in_dim(array, 0, width, axis=dim)
        before = lax.ppermute(last, axis, up)
        after = lax.ppermute(initial, axis, down)
        array = jnp.concatenate([before, array, after], axis=dim)
    return array


def gelu_tanh(values):
    return jax.nn.gelu(values, approximate=True)


def expand_layer(features, expand_weight, expand_bias):
    return gelu_tanh(
        jnp.dot(features, expand_weight, preferred_element_type=jnp.float32) + expand_bias
    ).astype(jnp.bfloat16)


def depthwise(padded, depth_weight, depth_bias, row_count, col_count):
    accumulated = jnp.zeros((row_count, col_count, padded.shape[2]), jnp.float32) + depth_bias
    for row_shift in range(3):
        for col_shift in range(3):
            accumulated = (
                accumulated
                + padded[row_shift : row_shift + row_count, col_shift : col_shift + col_count]
                * depth_weight[row_shift, col_shift]
            )
    return gelu_tanh(accumulated).astype(jnp.bfloat16)


def layer_norm(features, norm_gain, norm_bias):
    values = features.astype(jnp.float32)
    mean_value = jnp.mean(values, axis=-1, keepdims=True)
    variance = jnp.mean((values - mean_value) ** 2, axis=-1, keepdims=True)
    return ((values - mean_value) * lax.rsqrt(variance + 1e-05) * norm_gain + norm_bias).astype(
        jnp.bfloat16
    )


def grid_bias(position_bias, grid_side):
    position = jnp.arange(grid_side * grid_side, dtype=jnp.int32)
    row_of = position // grid_side
    col_of = position % grid_side
    offset_index = (row_of[:, None] - row_of[None, :] + grid_side - 1) * (2 * grid_side - 1) + (
        col_of[:, None] - col_of[None, :] + grid_side - 1
    )
    return jnp.take(position_bias, offset_index, axis=1)


def attend(projected, table, head_count):
    group_count, tokens, triple = projected.shape
    channels = triple // 3
    head_size = channels // head_count
    split_parts = projected.reshape(group_count, tokens, 3, head_count, head_size)
    query_part = split_parts[:, :, 0]
    key_part = split_parts[:, :, 1]
    value_part = split_parts[:, :, 2]
    scores = (
        jnp.einsum("nqhd,nkhd->nhqk", query_part, key_part, preferred_element_type=jnp.float32)
        * head_size ** (-0.5)
        + table[None]
    )
    probs = jax.nn.softmax(scores, axis=-1).astype(jnp.bfloat16)
    attended = jnp.einsum("nhqk,nkhd->nqhd", probs, value_part, preferred_element_type=jnp.float32)
    return attended.astype(jnp.bfloat16).reshape(group_count, tokens, channels)


def attention_kernel(x_ref, w_ref, bias_ref, o_ref):
    block, tokens, channels = x_ref.shape
    head_size = channels // HEADS
    x = x_ref[...].reshape(block * tokens, channels)
    qkv = jnp.dot(x, w_ref[...], preferred_element_type=jnp.float32).astype(jnp.bfloat16)
    query = qkv[:, :channels]
    key = qkv[:, channels : 2 * channels].reshape(block, tokens, channels)
    value = qkv[:, 2 * channels :]
    head_of = lax.broadcasted_iota(jnp.int32, (1, channels), 1) // head_size
    out = jnp.zeros((block, tokens, channels), jnp.float32)
    for head in range(HEADS):
        mask = head_of == head
        masked_query = jnp.where(mask, query, jnp.zeros_like(query)).reshape(block, tokens, channels)
        scores = (
            jnp.einsum("gtd,gud->gtu", masked_query, key, preferred_element_type=jnp.float32)
            * head_size ** (-0.5)
            + bias_ref[head][None]
        )
        shifted = jnp.exp(scores - jnp.max(scores, axis=-1, keepdims=True))
        probs = (shifted / jnp.sum(shifted, axis=-1, keepdims=True)).astype(jnp.bfloat16)
        masked_value = jnp.where(mask, value, jnp.zeros_like(value)).reshape(block, tokens, channels)
        part = jnp.einsum("gtu,gud->gtd", probs, masked_value, preferred_element_type=jnp.float32)
        out = jnp.where(mask.reshape(1, 1, channels), part, out)
    o_ref[...] = out.astype(o_ref.dtype)


def grid_attention(grouped, mixing_weight, table):
    count, tokens, channels = grouped.shape
    block = next(b for b in (32, 16, 8, 4, 2, 1) if count % b == 0)
    return pl.pallas_call(
        attention_kernel,
        grid=(count // block,),
        in_specs=[
            pl.BlockSpec((block, tokens, channels), lambda i: (i, 0, 0)),
            pl.BlockSpec(mixing_weight.shape, lambda i: (0, 0)),
            pl.BlockSpec(table.shape, lambda i: (0, 0, 0)),
        ],
        out_specs=pl.BlockSpec((block, tokens, channels), lambda i: (i, 0, 0)),
        out_shape=jax.ShapeDtypeStruct((count, tokens, channels), jnp.bfloat16),
    )(grouped, mixing_weight, table)


def pieces_of(normed, row_size, col_size, pp, span, col_count, channels):
    across = G // col_size
    inner_cols = col_count // across // col_size
    return (
        normed.reshape(row_size, pp, across, col_size, inner_cols, channels)
        .transpose(0, 3, 1, 2, 4, 5)
        .reshape(row_size * col_size, pp, across, inner_cols, channels)
    )


def expanded_window(sky_map, expand_weight, expand_bias, edges, first, span):
    top, bottom, left, right = edges
    row_count = sky_map.shape[0]
    low, high = first - 1, first + span + 1
    core = expand_layer(sky_map[max(low, 0) : min(high, row_count)], expand_weight, expand_bias)
    rows = jnp.concatenate(
        ([top] if low < 0 else []) + [core] + ([bottom] if high > row_count else []), axis=0
    )
    return jnp.concatenate(
        [left[first : first + span + 2], rows, right[first : first + span + 2]], axis=1
    )


def expanded_edges(sky_map, expand_weight, expand_bias):
    row_size, col_size = lax.axis_size("row"), lax.axis_size("col")
    row_at, col_at = lax.axis_index("row"), lax.axis_index("col")
    row_count = sky_map.shape[0]
    up = [(i, i + 1) for i in range(row_size - 1)]
    top = lax.ppermute(sky_map[row_count - 1], "row", up)[None]
    bottom = lax.ppermute(sky_map[0], "row", [(j, i) for i, j in up])[None]
    last_col = jnp.concatenate([top[:, -1], sky_map[:, -1], bottom[:, -1]], axis=0)
    first_col = jnp.concatenate([top[:, 0], sky_map[:, 0], bottom[:, 0]], axis=0)
    right_of = [(i, i + 1) for i in range(col_size - 1)]
    left = lax.ppermute(last_col, "col", right_of)[:, None]
    right = lax.ppermute(first_col, "col", [(j, i) for i, j in right_of])[:, None]
    row_ok = jnp.concatenate(
        [
            jnp.full((1,), row_at > 0),
            jnp.full((row_count,), True),
            jnp.full((1,), row_at < row_size - 1),
        ]
    )[:, None, None]

    def grown(cells, valid):
        return jnp.where(valid, expand_layer(cells, expand_weight, expand_bias), jnp.zeros((), jnp.bfloat16))

    return (
        grown(top, row_at > 0),
        grown(bottom, row_at < row_size - 1),
        grown(left, row_ok & (col_at > 0)),
        grown(right, row_ok & (col_at < col_size - 1)),
    )


def body(
    sky_map,
    expand_weight,
    expand_bias,
    depth_weight,
    depth_bias,
    project_weight,
    project_bias,
    norm_gain,
    norm_bias,
    mixing_weight,
    position_bias,
    output_weight,
):
    row_count, col_count, channels = sky_map.shape
    row_size = lax.axis_size("row")
    edges = expanded_edges(sky_map, expand_weight, expand_bias)
    across = G // lax.axis_size("col")
    stride = col_count // across
    table = grid_bias(position_bias, G)
    pieces = 2 if row_count % (2 * row_size) == 0 and (row_count // 2) % G == 0 else 1
    span = row_count // pieces
    col_size = lax.axis_size("col")
    sub = row_size // G
    pp = span // row_size
    inner_cols = stride // col_size
    source = sky_map
    outs = []
    for piece in range(pieces):
        first = piece * span
        window = expanded_window(source, expand_weight, expand_bias, edges, first, span)
        hidden = depthwise(window, depth_weight, depth_bias, span, col_count)
        after_conv = (
            sky_map[first : first + span].astype(jnp.float32)
            + jnp.dot(hidden, project_weight, preferred_element_type=jnp.float32)
            + project_bias
        ).astype(jnp.bfloat16)
        normed = layer_norm(after_conv, norm_gain, norm_bias)
        pair = pieces_of(normed, row_size, col_size, pp, span, col_count, channels)
        if piece + 1 < pieces:
            pair, source = lax.optimization_barrier((pair, sky_map))
        moved = lax.all_to_all(pair, ("row", "col"), 0, 0, tiled=True)
        grouped = (
            moved.reshape(G, sub, col_size, pp, across, inner_cols, channels)
            .transpose(1, 3, 5, 0, 2, 4, 6)
            .reshape(sub * pp * inner_cols, G * G, channels)
        )
        heads_out = grid_attention(grouped, mixing_weight, table)
        returned = (
            heads_out.reshape(sub, pp, inner_cols, G, col_size, across, channels)
            .transpose(3, 0, 4, 1, 5, 2, 6)
            .reshape(row_size * col_size, pp, across, inner_cols, channels)
        )
        returned = lax.all_to_all(returned, ("row", "col"), 0, 0, tiled=True)
        returned = (
            returned.reshape(row_size, col_size, pp, across, inner_cols, channels)
            .transpose(0, 2, 3, 1, 4, 5)
            .reshape(span, col_count, channels)
        )
        outs.append(
            (
                after_conv.astype(jnp.float32)
                + jnp.dot(returned, output_weight, preferred_element_type=jnp.float32)
            ).astype(jnp.bfloat16)
        )
    return jnp.concatenate(outs, axis=0)


def solution(mesh):
    placed = (
        P(("groups", "row"), "col", None),
        P(),
        P(),
        P(),
        P(),
        P(),
        P(),
        P(),
        P(),
        P(),
        P(),
        P(),
    )
    return jax.shard_map(
        body,
        mesh=mesh,
        in_specs=placed,
        out_specs=P(("groups", "row"), "col", None),
        check_vma=False,
    )
```

```python
import jax
import jax.numpy as jnp
from jax import lax
from jax.sharding import PartitionSpec as P
from jax.experimental import pallas as pl

HEADS = 4
G = 8


def with_halo(array, sides, width):
    for axis, dim in sides:
        size, length = (lax.axis_size(axis), array.shape[dim])
        up = [(i, (i + 1) % size) for i in range(size - 1)]
        down = [(j, i) for i, j in up]
        last = lax.slice_in_dim(array, length - width, length, axis=dim)
        initial = lax.slice_in_dim(array, 0, width, axis=dim)
        before = lax.ppermute(last, axis, up)
        after = lax.ppermute(initial, axis, down)
        array = jnp.concatenate([before, array, after], axis=dim)
    return array


def gelu_tanh(values):
    return jax.nn.gelu(values, approximate=True)


def expand_layer(features, expand_weight, expand_bias):
    return gelu_tanh(
        jnp.dot(features, expand_weight, preferred_element_type=jnp.float32) + expand_bias
    ).astype(jnp.bfloat16)


def depthwise(padded, depth_weight, depth_bias, row_count, col_count):
    accumulated = jnp.zeros((row_count, col_count, padded.shape[2]), jnp.float32) + depth_bias
    for row_shift in range(3):
        for col_shift in range(3):
            accumulated = (
                accumulated
                + padded[row_shift : row_shift + row_count, col_shift : col_shift + col_count]
                * depth_weight[row_shift, col_shift]
            )
    return gelu_tanh(accumulated).astype(jnp.bfloat16)


def layer_norm(features, norm_gain, norm_bias):
    values = features.astype(jnp.float32)
    mean_value = jnp.mean(values, axis=-1, keepdims=True)
    variance = jnp.mean((values - mean_value) ** 2, axis=-1, keepdims=True)
    return ((values - mean_value) * lax.rsqrt(variance + 1e-05) * norm_gain + norm_bias).astype(
        jnp.bfloat16
    )


def grid_bias(position_bias, grid_side):
    position = jnp.arange(grid_side * grid_side, dtype=jnp.int32)
    row_of = position // grid_side
    col_of = position % grid_side
    offset_index = (row_of[:, None] - row_of[None, :] + grid_side - 1) * (2 * grid_side - 1) + (
        col_of[:, None] - col_of[None, :] + grid_side - 1
    )
    return jnp.take(position_bias, offset_index, axis=1)


def attend(projected, table, head_count):
    group_count, tokens, triple = projected.shape
    channels = triple // 3
    head_size = channels // head_count
    split_parts = projected.reshape(group_count, tokens, 3, head_count, head_size)
    query_part = split_parts[:, :, 0]
    key_part = split_parts[:, :, 1]
    value_part = split_parts[:, :, 2]
    scores = (
        jnp.einsum("nqhd,nkhd->nhqk", query_part, key_part, preferred_element_type=jnp.float32)
        * head_size ** (-0.5)
        + table[None]
    )
    probs = jax.nn.softmax(scores, axis=-1).astype(jnp.bfloat16)
    attended = jnp.einsum("nhqk,nkhd->nqhd", probs, value_part, preferred_element_type=jnp.float32)
    return attended.astype(jnp.bfloat16).reshape(group_count, tokens, channels)


def attention_kernel(x_ref, w_ref, bias_ref, o_ref):
    block, tokens, channels = x_ref.shape
    head_size = channels // HEADS
    x = x_ref[...].reshape(block * tokens, channels)
    qkv = jnp.dot(x, w_ref[...], preferred_element_type=jnp.float32).astype(jnp.bfloat16)
    query = qkv[:, :channels]
    key = qkv[:, channels : 2 * channels].reshape(block, tokens, channels)
    value = qkv[:, 2 * channels :]
    head_of = lax.broadcasted_iota(jnp.int32, (1, channels), 1) // head_size
    out = jnp.zeros((block, tokens, channels), jnp.float32)
    for head in range(HEADS):
        mask = head_of == head
        masked_query = jnp.where(mask, query, jnp.zeros_like(query)).reshape(block, tokens, channels)
        scores = (
            jnp.einsum("gtd,gud->gtu", masked_query, key, preferred_element_type=jnp.float32)
            * head_size ** (-0.5)
            + bias_ref[head][None]
        )
        shifted = jnp.exp(scores - jnp.max(scores, axis=-1, keepdims=True))
        probs = (shifted / jnp.sum(shifted, axis=-1, keepdims=True)).astype(jnp.bfloat16)
        masked_value = jnp.where(mask, value, jnp.zeros_like(value)).reshape(block, tokens, channels)
        part = jnp.einsum("gtu,gud->gtd", probs, masked_value, preferred_element_type=jnp.float32)
        out = jnp.where(mask.reshape(1, 1, channels), part, out)
    o_ref[...] = out.astype(o_ref.dtype)


def grid_attention(grouped, mixing_weight, table):
    count, tokens, channels = grouped.shape
    block = next(b for b in (32, 16, 8, 4, 2, 1) if count % b == 0)
    return pl.pallas_call(
        attention_kernel,
        grid=(count // block,),
        in_specs=[
            pl.BlockSpec((block, tokens, channels), lambda i: (i, 0, 0)),
            pl.BlockSpec(mixing_weight.shape, lambda i: (0, 0)),
            pl.BlockSpec(table.shape, lambda i: (0, 0, 0)),
        ],
        out_specs=pl.BlockSpec((block, tokens, channels), lambda i: (i, 0, 0)),
        out_shape=jax.ShapeDtypeStruct((count, tokens, channels), jnp.bfloat16),
    )(grouped, mixing_weight, table)


def pieces_of(normed, row_size, col_size, pp, span, col_count, channels):
    across = G // col_size
    inner_cols = col_count // across // col_size
    return (
        normed.reshape(row_size, pp, across, col_size, inner_cols, channels)
        .transpose(0, 3, 1, 2, 4, 5)
        .reshape(row_size * col_size, pp, across, inner_cols, channels)
    )


def expanded_window(expanded, edges, first, span):
    top, bottom, left, right = edges
    rows = jnp.concatenate([top, expanded, bottom], axis=0)[first : first + span + 2]
    return jnp.concatenate(
        [left[first : first + span + 2], rows, right[first : first + span + 2]], axis=1
    )


def expanded_edges(sky_map, expand_weight, expand_bias):
    row_size, col_size = lax.axis_size("row"), lax.axis_size("col")
    row_at, col_at = lax.axis_index("row"), lax.axis_index("col")
    row_count = sky_map.shape[0]
    up = [(i, i + 1) for i in range(row_size - 1)]
    top = lax.ppermute(sky_map[row_count - 1], "row", up)[None]
    bottom = lax.ppermute(sky_map[0], "row", [(j, i) for i, j in up])[None]
    last_col = jnp.concatenate([top[:, -1], sky_map[:, -1], bottom[:, -1]], axis=0)
    first_col = jnp.concatenate([top[:, 0], sky_map[:, 0], bottom[:, 0]], axis=0)
    right_of = [(i, i + 1) for i in range(col_size - 1)]
    left = lax.ppermute(last_col, "col", right_of)[:, None]
    right = lax.ppermute(first_col, "col", [(j, i) for i, j in right_of])[:, None]
    row_ok = jnp.concatenate(
        [
            jnp.full((1,), row_at > 0),
            jnp.full((row_count,), True),
            jnp.full((1,), row_at < row_size - 1),
        ]
    )[:, None, None]

    def grown(cells, valid):
        return jnp.where(valid, expand_layer(cells, expand_weight, expand_bias), jnp.zeros((), jnp.bfloat16))

    return (
        grown(top, row_at > 0),
        grown(bottom, row_at < row_size - 1),
        grown(left, row_ok & (col_at > 0)),
        grown(right, row_ok & (col_at < col_size - 1)),
    )


def body(
    sky_map,
    expand_weight,
    expand_bias,
    depth_weight,
    depth_bias,
    project_weight,
    project_bias,
    norm_gain,
    norm_bias,
    mixing_weight,
    position_bias,
    output_weight,
):
    row_count, col_count, channels = sky_map.shape
    row_size = lax.axis_size("row")
    expanded = expand_layer(sky_map, expand_weight, expand_bias)
    edges = expanded_edges(sky_map, expand_weight, expand_bias)
    across = G // lax.axis_size("col")
    stride = col_count // across
    table = grid_bias(position_bias, G)
    pieces = 2 if row_count % (2 * row_size) == 0 and (row_count // 2) % G == 0 else 1
    span = row_count // pieces
    col_size = lax.axis_size("col")
    sub = row_size // G
    pp = span // row_size
    inner_cols = stride // col_size
    source = expanded
    outs = []
    for piece in range(pieces):
        first = piece * span
        window = expanded_window(source, edges, first, span)
        hidden = depthwise(window, depth_weight, depth_bias, span, col_count)
        after_conv = (
            sky_map[first : first + span].astype(jnp.float32)
            + jnp.dot(hidden, project_weight, preferred_element_type=jnp.float32)
            + project_bias
        ).astype(jnp.bfloat16)
        normed = layer_norm(after_conv, norm_gain, norm_bias)
        pair = pieces_of(normed, row_size, col_size, pp, span, col_count, channels)
        if piece + 1 < pieces:
            pair, source = lax.optimization_barrier((pair, expanded))
        moved = lax.all_to_all(pair, ("row", "col"), 0, 0, tiled=True)
        grouped = (
            moved.reshape(G, sub, col_size, pp, across, inner_cols, channels)
            .transpose(1, 3, 5, 0, 2, 4, 6)
            .reshape(sub * pp * inner_cols, G * G, channels)
        )
        heads_out = grid_attention(grouped, mixing_weight, table)
        returned = (
            heads_out.reshape(sub, pp, inner_cols, G, col_size, across, channels)
            .transpose(3, 0, 4, 1, 5, 2, 6)
            .reshape(row_size * col_size, pp, across, inner_cols, channels)
        )
        returned = lax.all_to_all(returned, ("row", "col"), 0, 0, tiled=True)
        returned = (
            returned.reshape(row_size, col_size, pp, across, inner_cols, channels)
            .transpose(0, 2, 3, 1, 4, 5)
            .reshape(span, col_count, channels)
        )
        outs.append((after_conv, returned))
    after_conv = jnp.concatenate([a for a, _ in outs], axis=0)
    returned = jnp.concatenate([r for _, r in outs], axis=0)
    return (
        after_conv.astype(jnp.float32)
        + jnp.dot(returned, output_weight, preferred_element_type=jnp.float32)
    ).astype(jnp.bfloat16)


def solution(mesh):
    placed = (
        P(("groups", "row"), "col", None),
        P(),
        P(),
        P(),
        P(),
        P(),
        P(),
        P(),
        P(),
        P(),
        P(),
        P(),
    )
    return jax.shard_map(
        body,
        mesh=mesh,
        in_specs=placed,
        out_specs=P(("groups", "row"), "col", None),
        check_vma=False,
    )
```

```python
import jax
import jax.numpy as jnp
from jax import lax
from jax.sharding import PartitionSpec as P
from jax.experimental import pallas as pl

HEADS = 4
G = 8


def with_halo(array, sides, width):
    for axis, dim in sides:
        size, length = (lax.axis_size(axis), array.shape[dim])
        up = [(i, (i + 1) % size) for i in range(size - 1)]
        down = [(j, i) for i, j in up]
        last = lax.slice_in_dim(array, length - width, length, axis=dim)
        initial = lax.slice_in_dim(array, 0, width, axis=dim)
        before = lax.ppermute(last, axis, up)
        after = lax.ppermute(initial, axis, down)
        array = jnp.concatenate([before, array, after], axis=dim)
    return array


def gelu_tanh(values):
    return jax.nn.gelu(values, approximate=True)


def expand_layer(features, expand_weight, expand_bias):
    return gelu_tanh(
        jnp.dot(features, expand_weight, preferred_element_type=jnp.float32) + expand_bias
    ).astype(jnp.bfloat16)


def depthwise(padded, depth_weight, depth_bias, row_count, col_count):
    accumulated = jnp.zeros((row_count, col_count, padded.shape[2]), jnp.float32) + depth_bias
    for row_shift in range(3):
        for col_shift in range(3):
            accumulated = (
                accumulated
                + padded[row_shift : row_shift + row_count, col_shift : col_shift + col_count]
                * depth_weight[row_shift, col_shift]
            )
    return gelu_tanh(accumulated).astype(jnp.bfloat16)


def layer_norm(features, norm_gain, norm_bias):
    values = features.astype(jnp.float32)
    mean_value = jnp.mean(values, axis=-1, keepdims=True)
    variance = jnp.mean((values - mean_value) ** 2, axis=-1, keepdims=True)
    return ((values - mean_value) * lax.rsqrt(variance + 1e-05) * norm_gain + norm_bias).astype(
        jnp.bfloat16
    )


def grid_bias(position_bias, grid_side):
    span = 2 * grid_side - 1
    place = jnp.arange(grid_side, dtype=jnp.int32)
    offset = (place[:, None] - place[None, :] + grid_side - 1).reshape(-1)
    pick = (offset[:, None] == jnp.arange(span, dtype=jnp.int32)[None, :]).astype(jnp.float32)
    grid = position_bias.reshape(-1, span, span)
    table = jnp.einsum("xa,hab,yb->hxy", pick, grid, pick, precision=lax.Precision.HIGHEST)
    return (
        table.reshape(-1, grid_side, grid_side, grid_side, grid_side)
        .transpose(0, 1, 3, 2, 4)
        .reshape(-1, grid_side * grid_side, grid_side * grid_side)
    )


def attend(projected, table, head_count):
    group_count, tokens, triple = projected.shape
    channels = triple // 3
    head_size = channels // head_count
    split_parts = projected.reshape(group_count, tokens, 3, head_count, head_size)
    query_part = split_parts[:, :, 0]
    key_part = split_parts[:, :, 1]
    value_part = split_parts[:, :, 2]
    scores = (
        jnp.einsum("nqhd,nkhd->nhqk", query_part, key_part, preferred_element_type=jnp.float32)
        * head_size ** (-0.5)
        + table[None]
    )
    probs = jax.nn.softmax(scores, axis=-1).astype(jnp.bfloat16)
    attended = jnp.einsum("nhqk,nkhd->nqhd", probs, value_part, preferred_element_type=jnp.float32)
    return attended.astype(jnp.bfloat16).reshape(group_count, tokens, channels)


def attention_kernel(x_ref, w_ref, bias_ref, o_ref):
    block, tokens, channels = x_ref.shape
    head_size = channels // HEADS
    x = x_ref[...].reshape(block * tokens, channels)
    qkv = jnp.dot(x, w_ref[...], preferred_element_type=jnp.float32).astype(jnp.bfloat16)
    query = qkv[:, :channels]
    key = qkv[:, channels : 2 * channels].reshape(block, tokens, channels)
    value = qkv[:, 2 * channels :]
    head_of = lax.broadcasted_iota(jnp.int32, (1, channels), 1) // head_size
    out = jnp.zeros((block, tokens, channels), jnp.float32)
    for head in range(HEADS):
        mask = head_of == head
        masked_query = jnp.where(mask, query, jnp.zeros_like(query)).reshape(block, tokens, channels)
        scores = (
            jnp.einsum("gtd,gud->gtu", masked_query, key, preferred_element_type=jnp.float32)
            * head_size ** (-0.5)
            + bias_ref[head][None]
        )
        shifted = jnp.exp(scores - jnp.max(scores, axis=-1, keepdims=True))
        probs = (shifted / jnp.sum(shifted, axis=-1, keepdims=True)).astype(jnp.bfloat16)
        masked_value = jnp.where(mask, value, jnp.zeros_like(value)).reshape(block, tokens, channels)
        part = jnp.einsum("gtu,gud->gtd", probs, masked_value, preferred_element_type=jnp.float32)
        out = jnp.where(mask.reshape(1, 1, channels), part, out)
    o_ref[...] = out.astype(o_ref.dtype)


def grid_attention(grouped, mixing_weight, table):
    count, tokens, channels = grouped.shape
    block = next(b for b in (32, 16, 8, 4, 2, 1) if count % b == 0)
    return pl.pallas_call(
        attention_kernel,
        grid=(count // block,),
        in_specs=[
            pl.BlockSpec((block, tokens, channels), lambda i: (i, 0, 0)),
            pl.BlockSpec(mixing_weight.shape, lambda i: (0, 0)),
            pl.BlockSpec(table.shape, lambda i: (0, 0, 0)),
        ],
        out_specs=pl.BlockSpec((block, tokens, channels), lambda i: (i, 0, 0)),
        out_shape=jax.ShapeDtypeStruct((count, tokens, channels), jnp.bfloat16),
    )(grouped, mixing_weight, table)


def pieces_of(normed, row_size, col_size, pp, span, col_count, channels):
    across = G // col_size
    inner_cols = col_count // across // col_size
    return (
        normed.reshape(row_size, pp, across, col_size, inner_cols, channels)
        .transpose(0, 3, 1, 2, 4, 5)
        .reshape(row_size * col_size, pp, across, inner_cols, channels)
    )


def expanded_window(expanded, edges, first, span):
    top, bottom, left, right = edges
    rows = jnp.concatenate([top, expanded, bottom], axis=0)[first : first + span + 2]
    return jnp.concatenate(
        [left[first : first + span + 2], rows, right[first : first + span + 2]], axis=1
    )


def expanded_edges(sky_map, expand_weight, expand_bias):
    row_size, col_size = lax.axis_size("row"), lax.axis_size("col")
    row_at, col_at = lax.axis_index("row"), lax.axis_index("col")
    row_count = sky_map.shape[0]
    up = [(i, i + 1) for i in range(row_size - 1)]
    top = lax.ppermute(sky_map[row_count - 1], "row", up)[None]
    bottom = lax.ppermute(sky_map[0], "row", [(j, i) for i, j in up])[None]
    last_col = jnp.concatenate([top[:, -1], sky_map[:, -1], bottom[:, -1]], axis=0)
    first_col = jnp.concatenate([top[:, 0], sky_map[:, 0], bottom[:, 0]], axis=0)
    right_of = [(i, i + 1) for i in range(col_size - 1)]
    left = lax.ppermute(last_col, "col", right_of)[:, None]
    right = lax.ppermute(first_col, "col", [(j, i) for i, j in right_of])[:, None]
    row_ok = jnp.concatenate(
        [
            jnp.full((1,), row_at > 0),
            jnp.full((row_count,), True),
            jnp.full((1,), row_at < row_size - 1),
        ]
    )[:, None, None]

    def grown(cells, valid):
        return jnp.where(valid, expand_layer(cells, expand_weight, expand_bias), jnp.zeros((), jnp.bfloat16))

    return (
        grown(top, row_at > 0),
        grown(bottom, row_at < row_size - 1),
        grown(left, row_ok & (col_at > 0)),
        grown(right, row_ok & (col_at < col_size - 1)),
    )


def body(
    sky_map,
    expand_weight,
    expand_bias,
    depth_weight,
    depth_bias,
    project_weight,
    project_bias,
    norm_gain,
    norm_bias,
    mixing_weight,
    position_bias,
    output_weight,
):
    row_count, col_count, channels = sky_map.shape
    row_size = lax.axis_size("row")
    expanded = expand_layer(sky_map, expand_weight, expand_bias)
    edges = expanded_edges(sky_map, expand_weight, expand_bias)
    across = G // lax.axis_size("col")
    stride = col_count // across
    table = grid_bias(position_bias, G)
    pieces = 2 if row_count % (2 * row_size) == 0 and (row_count // 2) % G == 0 else 1
    span = row_count // pieces
    col_size = lax.axis_size("col")
    sub = row_size // G
    pp = span // row_size
    inner_cols = stride // col_size
    source = expanded
    outs = []
    for piece in range(pieces):
        first = piece * span
        window = expanded_window(source, edges, first, span)
        hidden = depthwise(window, depth_weight, depth_bias, span, col_count)
        after_conv = (
            sky_map[first : first + span].astype(jnp.float32)
            + jnp.dot(hidden, project_weight, preferred_element_type=jnp.float32)
            + project_bias
        ).astype(jnp.bfloat16)
        normed = layer_norm(after_conv, norm_gain, norm_bias)
        pair = pieces_of(normed, row_size, col_size, pp, span, col_count, channels)
        if piece + 1 < pieces:
            pair, source = lax.optimization_barrier((pair, expanded))
        moved = lax.all_to_all(pair, ("row", "col"), 0, 0, tiled=True)
        grouped = (
            moved.reshape(G, sub, col_size, pp, across, inner_cols, channels)
            .transpose(1, 3, 5, 0, 2, 4, 6)
            .reshape(sub * pp * inner_cols, G * G, channels)
        )
        heads_out = grid_attention(grouped, mixing_weight, table)
        returned = (
            heads_out.reshape(sub, pp, inner_cols, G, col_size, across, channels)
            .transpose(3, 0, 4, 1, 5, 2, 6)
            .reshape(row_size * col_size, pp, across, inner_cols, channels)
        )
        returned = lax.all_to_all(returned, ("row", "col"), 0, 0, tiled=True)
        returned = (
            returned.reshape(row_size, col_size, pp, across, inner_cols, channels)
            .transpose(0, 2, 3, 1, 4, 5)
            .reshape(span, col_count, channels)
        )
        outs.append(
            (
                after_conv.astype(jnp.float32)
                + jnp.dot(returned, output_weight, preferred_element_type=jnp.float32)
            ).astype(jnp.bfloat16)
        )
    return jnp.concatenate(outs, axis=0)


def solution(mesh):
    placed = (
        P(("groups", "row"), "col", None),
        P(),
        P(),
        P(),
        P(),
        P(),
        P(),
        P(),
        P(),
        P(),
        P(),
        P(),
    )
    return jax.shard_map(
        body,
        mesh=mesh,
        in_specs=placed,
        out_specs=P(("groups", "row"), "col", None),
        check_vma=False,
    )
```

```python
import jax
import jax.numpy as jnp
from jax import lax
from jax.sharding import PartitionSpec as P
from jax.experimental import pallas as pl

HEADS = 4
G = 8


def with_halo(array, sides, width):
    for axis, dim in sides:
        size, length = (lax.axis_size(axis), array.shape[dim])
        up = [(i, (i + 1) % size) for i in range(size - 1)]
        down = [(j, i) for i, j in up]
        last = lax.slice_in_dim(array, length - width, length, axis=dim)
        initial = lax.slice_in_dim(array, 0, width, axis=dim)
        before = lax.ppermute(last, axis, up)
        after = lax.ppermute(initial, axis, down)
        array = jnp.concatenate([before, array, after], axis=dim)
    return array


def gelu_tanh(values):
    return jax.nn.gelu(values, approximate=True)


def expand_layer(features, expand_weight, expand_bias):
    return gelu_tanh(
        jnp.dot(features, expand_weight, preferred_element_type=jnp.float32) + expand_bias
    ).astype(jnp.bfloat16)


def depthwise(padded, depth_weight, depth_bias, row_count, col_count):
    accumulated = jnp.zeros((row_count, col_count, padded.shape[2]), jnp.float32) + depth_bias
    for row_shift in range(3):
        for col_shift in range(3):
            accumulated = (
                accumulated
                + padded[row_shift : row_shift + row_count, col_shift : col_shift + col_count]
                * depth_weight[row_shift, col_shift]
            )
    return gelu_tanh(accumulated).astype(jnp.bfloat16)


def layer_norm(features, norm_gain, norm_bias):
    values = features.astype(jnp.float32)
    mean_value = jnp.mean(values, axis=-1, keepdims=True)
    variance = jnp.mean((values - mean_value) ** 2, axis=-1, keepdims=True)
    return ((values - mean_value) * lax.rsqrt(variance + 1e-05) * norm_gain + norm_bias).astype(
        jnp.bfloat16
    )


def grid_bias(position_bias, grid_side):
    position = jnp.arange(grid_side * grid_side, dtype=jnp.int32)
    row_of = position // grid_side
    col_of = position % grid_side
    offset_index = (row_of[:, None] - row_of[None, :] + grid_side - 1) * (2 * grid_side - 1) + (
        col_of[:, None] - col_of[None, :] + grid_side - 1
    )
    return jnp.take(position_bias, offset_index, axis=1)


def attend(projected, table, head_count):
    group_count, tokens, triple = projected.shape
    channels = triple // 3
    head_size = channels // head_count
    split_parts = projected.reshape(group_count, tokens, 3, head_count, head_size)
    query_part = split_parts[:, :, 0]
    key_part = split_parts[:, :, 1]
    value_part = split_parts[:, :, 2]
    scores = (
        jnp.einsum("nqhd,nkhd->nhqk", query_part, key_part, preferred_element_type=jnp.float32)
        * head_size ** (-0.5)
        + table[None]
    )
    probs = jax.nn.softmax(scores, axis=-1).astype(jnp.bfloat16)
    attended = jnp.einsum("nhqk,nkhd->nqhd", probs, value_part, preferred_element_type=jnp.float32)
    return attended.astype(jnp.bfloat16).reshape(group_count, tokens, channels)


def attention_kernel(x_ref, w_ref, bias_ref, o_ref):
    block, tokens, channels = x_ref.shape
    head_size = channels // HEADS
    x = x_ref[...].reshape(block * tokens, channels)
    qkv = jnp.dot(x, w_ref[...], preferred_element_type=jnp.float32).astype(jnp.bfloat16)
    query = qkv[:, :channels]
    key = qkv[:, channels : 2 * channels].reshape(block, tokens, channels)
    value = qkv[:, 2 * channels :]
    head_of = lax.broadcasted_iota(jnp.int32, (1, channels), 1) // head_size
    out = jnp.zeros((block, tokens, channels), jnp.float32)
    for head in range(HEADS):
        mask = head_of == head
        masked_query = jnp.where(mask, query, jnp.zeros_like(query)).reshape(block, tokens, channels)
        scores = (
            jnp.einsum("gtd,gud->gtu", masked_query, key, preferred_element_type=jnp.float32)
            * head_size ** (-0.5)
            + bias_ref[head][None]
        )
        shifted = jnp.exp(scores - jnp.max(scores, axis=-1, keepdims=True))
        probs = (shifted / jnp.sum(shifted, axis=-1, keepdims=True)).astype(jnp.bfloat16)
        masked_value = jnp.where(mask, value, jnp.zeros_like(value)).reshape(block, tokens, channels)
        part = jnp.einsum("gtu,gud->gtd", probs, masked_value, preferred_element_type=jnp.float32)
        out = jnp.where(mask.reshape(1, 1, channels), part, out)
    o_ref[...] = out.astype(o_ref.dtype)


def grid_attention(grouped, mixing_weight, table):
    count, tokens, channels = grouped.shape
    block = next(b for b in (32, 16, 8, 4, 2, 1) if count % b == 0)
    return pl.pallas_call(
        attention_kernel,
        grid=(count // block,),
        in_specs=[
            pl.BlockSpec((block, tokens, channels), lambda i: (i, 0, 0)),
            pl.BlockSpec(mixing_weight.shape, lambda i: (0, 0)),
            pl.BlockSpec(table.shape, lambda i: (0, 0, 0)),
        ],
        out_specs=pl.BlockSpec((block, tokens, channels), lambda i: (i, 0, 0)),
        out_shape=jax.ShapeDtypeStruct((count, tokens, channels), jnp.bfloat16),
    )(grouped, mixing_weight, table)


def pieces_of(normed, row_size, col_size, pp, span, col_count, channels):
    across = G // col_size
    inner_cols = col_count // across // col_size
    return (
        normed.reshape(row_size, pp, across, col_size, inner_cols, channels)
        .transpose(0, 3, 1, 2, 4, 5)
        .reshape(row_size * col_size, pp, across, inner_cols, channels)
    )


def expanded_window(expanded, edges, first, span):
    top, bottom, left, right = edges
    rows = jnp.concatenate([top, expanded, bottom], axis=0)[first : first + span + 2]
    return jnp.concatenate(
        [left[first : first + span + 2], rows, right[first : first + span + 2]], axis=1
    )


def expanded_edges(sky_map, expand_weight, expand_bias):
    row_size, col_size = lax.axis_size("row"), lax.axis_size("col")
    row_at, col_at = lax.axis_index("row"), lax.axis_index("col")
    row_count = sky_map.shape[0]
    up = [(i, i + 1) for i in range(row_size - 1)]
    top = lax.ppermute(sky_map[row_count - 1], "row", up)[None]
    bottom = lax.ppermute(sky_map[0], "row", [(j, i) for i, j in up])[None]
    last_col = jnp.concatenate([top[:, -1], sky_map[:, -1], bottom[:, -1]], axis=0)
    first_col = jnp.concatenate([top[:, 0], sky_map[:, 0], bottom[:, 0]], axis=0)
    right_of = [(i, i + 1) for i in range(col_size - 1)]
    left = lax.ppermute(last_col, "col", right_of)[:, None]
    right = lax.ppermute(first_col, "col", [(j, i) for i, j in right_of])[:, None]
    row_ok = jnp.concatenate(
        [
            jnp.full((1,), row_at > 0),
            jnp.full((row_count,), True),
            jnp.full((1,), row_at < row_size - 1),
        ]
    )[:, None, None]

    width, height = top.shape[1], left.shape[0]
    cells = jnp.concatenate([top[0], bottom[0], left[:, 0], right[:, 0]], axis=0)
    grown = expand_layer(cells, expand_weight, expand_bias)
    zero = jnp.zeros((), jnp.bfloat16)
    return (
        jnp.where(row_at > 0, grown[:width], zero)[None],
        jnp.where(row_at < row_size - 1, grown[width : 2 * width], zero)[None],
        jnp.where(row_ok & (col_at > 0), grown[2 * width : 2 * width + height][:, None], zero),
        jnp.where(row_ok & (col_at < col_size - 1), grown[2 * width + height :][:, None], zero),
    )


def body(
    sky_map,
    expand_weight,
    expand_bias,
    depth_weight,
    depth_bias,
    project_weight,
    project_bias,
    norm_gain,
    norm_bias,
    mixing_weight,
    position_bias,
    output_weight,
):
    row_count, col_count, channels = sky_map.shape
    row_size = lax.axis_size("row")
    expanded = expand_layer(sky_map, expand_weight, expand_bias)
    edges = expanded_edges(sky_map, expand_weight, expand_bias)
    across = G // lax.axis_size("col")
    stride = col_count // across
    table = grid_bias(position_bias, G)
    pieces = 2 if row_count % (2 * row_size) == 0 and (row_count // 2) % G == 0 else 1
    span = row_count // pieces
    col_size = lax.axis_size("col")
    sub = row_size // G
    pp = span // row_size
    inner_cols = stride // col_size
    source = expanded
    outs = []
    for piece in range(pieces):
        first = piece * span
        window = expanded_window(source, edges, first, span)
        hidden = depthwise(window, depth_weight, depth_bias, span, col_count)
        after_conv = (
            sky_map[first : first + span].astype(jnp.float32)
            + jnp.dot(hidden, project_weight, preferred_element_type=jnp.float32)
            + project_bias
        ).astype(jnp.bfloat16)
        normed = layer_norm(after_conv, norm_gain, norm_bias)
        pair = pieces_of(normed, row_size, col_size, pp, span, col_count, channels)
        if piece + 1 < pieces:
            pair, source = lax.optimization_barrier((pair, expanded))
        moved = lax.all_to_all(pair, ("row", "col"), 0, 0, tiled=True)
        grouped = (
            moved.reshape(G, sub, col_size, pp, across, inner_cols, channels)
            .transpose(1, 3, 5, 0, 2, 4, 6)
            .reshape(sub * pp * inner_cols, G * G, channels)
        )
        heads_out = grid_attention(grouped, mixing_weight, table)
        returned = (
            heads_out.reshape(sub, pp, inner_cols, G, col_size, across, channels)
            .transpose(3, 0, 4, 1, 5, 2, 6)
            .reshape(row_size * col_size, pp, across, inner_cols, channels)
        )
        returned = lax.all_to_all(returned, ("row", "col"), 0, 0, tiled=True)
        returned = (
            returned.reshape(row_size, col_size, pp, across, inner_cols, channels)
            .transpose(0, 2, 3, 1, 4, 5)
            .reshape(span, col_count, channels)
        )
        outs.append(
            (
                after_conv.astype(jnp.float32)
                + jnp.dot(returned, output_weight, preferred_element_type=jnp.float32)
            ).astype(jnp.bfloat16)
        )
    return jnp.concatenate(outs, axis=0)


def solution(mesh):
    placed = (
        P(("groups", "row"), "col", None),
        P(),
        P(),
        P(),
        P(),
        P(),
        P(),
        P(),
        P(),
        P(),
        P(),
        P(),
    )
    return jax.shard_map(
        body,
        mesh=mesh,
        in_specs=placed,
        out_specs=P(("groups", "row"), "col", None),
        check_vma=False,
    )
```
